512 devices in a mesh: az: 64 (over z, y_lo, core), rad: 8 (over y_hi, x).
Axes of the slice: x: 4, y: 8 (y_hi: 2, y_lo: 4; y = y_hi * 4 + y_lo), z: 8, core: 2. Of those that a mesh axis runs over, the one named last changes fastest.
Arguments:
- density: float32 [1024, 384, 128], P('az', 'rad'), may hold values from 0.5 to 1.5
- flow_vars: float32 [4, 1024, 384, 128], P(None, 'az', 'rad'), may hold values from -6 to 6
- blade_offset: int32 [4], replicated, may hold values from 0 to 4, as said below
- smooth_width: int32 [128], replicated, may hold values from 1 to 4, as said below
Outputs:
- mean_fields: float32 [5, 1024, 384, 128], P(None, 'az', 'rad')
- q_field: float32 [1024, 384, 128], P('az', 'rad')
The draws below stay inside these ranges and needn't reach their ends.
Inputs may be any that keep to these rules, and one draw needn't show every extreme that they name: `blade_offset`: some blade's passage has the offset 4. `smooth_width`: some axial station uses the half-width 4.
All inputs are finite; a program needn't handle non-finite values.
Results may differ from the reference program's by a relative error of at most 0.00002.
Values sent between devices are 32-bit elements; how exact they have to be, the bound alone decides.
No kernel may reach another device: no remote copies, remote signals or barrier semaphores. Data moves between devices by JAX's collectives and lax.ppermute only.
A program may use at most 64 MiB of HBM per device.

```python
import math
import jax
import jax.numpy as jnp
from jax import lax

Z = 128
BLADES = 4
MAXOFF = 4
HW = 4
AZ = 1024
R = 384


def draw_blade_offset(key, part):
    base_key = jax.random.fold_in(key, 11)
    value_key, choose_key = jax.random.split(base_key)
    values = jax.random.randint(value_key, (BLADES,), 0, MAXOFF + 1, dtype=jnp.int32)
    chosen = jax.random.randint(choose_key, (), 0, BLADES, dtype=jnp.int32)
    return jnp.where(jnp.arange(BLADES, dtype=jnp.int32) == chosen, MAXOFF, values).astype(jnp.int32)


def draw_smooth_width(key, part):
    base_key = jax.random.fold_in(key, 23)
    value_key, choose_key = jax.random.split(base_key)
    values = jax.random.randint(value_key, (Z,), 1, HW + 1, dtype=jnp.int32)
    chosen = jax.random.randint(choose_key, (), 0, Z, dtype=jnp.int32)
    return jnp.where(jnp.arange(Z, dtype=jnp.int32) == chosen, HW, values).astype(jnp.int32)


def steps_of(rng, shape, pieces, low, high):
    def one(dim, parts):
        steps = jax.random.uniform(jax.random.fold_in(jax.random.fold_in(rng, 6), dim), (parts,), jnp.float32, low / len(pieces), high / len(pieces))
        return jnp.repeat(jnp.exp(steps), shape[dim] // parts).reshape((-1,) + (1,) * (len(shape) - dim - 1))

    level = one(*pieces[0])
    for cut in pieces[1:]:
        level = level * one(*cut)
    return level


def gaussian(key, dims, scale, reach, cuts=(), kind=jnp.bfloat16):
    result = jax.random.normal(key, dims, jnp.float32) * scale
    if len(cuts) > 0:
        result = steps_of(key, dims, cuts, -0.22, 0.18) * result
    return jnp.clip(result, min=-reach, max=reach).astype(kind)


def setup_inputs(seed: int = 0) -> dict:
    arg_keys = jax.random.split(jax.random.key(seed), 5)
    density = jnp.clip(0.5 + 1.0 * jax.random.uniform(arg_keys[0], (AZ, R, Z), jnp.float32) ** steps_of(arg_keys[0], (AZ, R, Z), ((0, 64), (1, 8)), -0.2, 0.2), 0.5, 1.5)
    flow_vars = gaussian(arg_keys[1], (4, AZ, R, Z), 1.0, 6.0, ((1, 64), (2, 8)), jnp.float32)
    blade_offset = draw_blade_offset(jax.random.fold_in(arg_keys[4], 71), 0)
    smooth_width = draw_smooth_width(jax.random.fold_in(arg_keys[4], 71), 0)
    return dict(density=density, flow_vars=flow_vars, blade_offset=blade_offset, smooth_width=smooth_width)


def smoothing_taps(smooth_width):
    spread = jnp.arange(-HW, HW + 1)
    width = smooth_width.astype(jnp.float32)
    square = (spread.astype(jnp.float32) ** 2)[:, None]
    weights = jnp.where(jnp.abs(spread)[:, None] <= smooth_width[None, :], jnp.exp(-0.5 * square / (width * width)[None, :]), 0.0)
    return weights / jnp.sum(weights, axis=0, keepdims=True)


def edge_rate(field, axis):
    count = field.shape[axis]
    upper = jnp.concatenate([lax.slice_in_dim(field, 1, count, axis=axis), lax.slice_in_dim(field, count - 1, count, axis=axis)], axis=axis)
    lower = jnp.concatenate([lax.slice_in_dim(field, 0, 1, axis=axis), lax.slice_in_dim(field, 0, count - 1, axis=axis)], axis=axis)
    places = jnp.arange(count)
    span = jnp.where((places == 0) | (places == count - 1), 1.0, 2.0).astype(field.dtype)
    layout = [1] * field.ndim
    layout[axis] = count
    return (upper - lower) / span.reshape(layout)


def swirl_measure(smoothed, az_rate, radial_rate, axial_rate, radius):
    tensor_aa = radial_rate[0]
    tensor_ab = (az_rate[0] - smoothed[1]) / radius
    tensor_ac = axial_rate[0]
    tensor_ba = radial_rate[1]
    tensor_bb = (az_rate[1] + smoothed[0]) / radius
    tensor_bc = axial_rate[1]
    tensor_ca = radial_rate[2]
    tensor_cb = az_rate[2] / radius
    tensor_cc = axial_rate[2]
    diagonal_part = tensor_aa * tensor_aa + tensor_bb * tensor_bb + tensor_cc * tensor_cc
    cross_part = tensor_ab * tensor_ba + tensor_ac * tensor_ca + tensor_bc * tensor_cb
    return -0.5 * (diagonal_part + 2.0 * cross_part)


def reference(density, flow_vars, blade_offset, smooth_width):
    velocity = flow_vars[0:3]
    carried = jnp.concatenate([density[None], density[None] * velocity, flow_vars[3:4]], axis=0)
    sector = AZ // BLADES
    phase = jnp.arange(sector).astype(jnp.int32)
    sector_sums = jnp.zeros((5, sector, R, Z), jnp.float32)
    for blade in range(BLADES):
        index = ((blade * sector + blade_offset[blade] + phase) % AZ).astype(jnp.int32)
        sector_sums = sector_sums + jnp.take(carried, index, axis=1)
    theta = jnp.arange(AZ).astype(jnp.int32)
    owner = (theta // sector).astype(jnp.int32)
    table_offset = jnp.take(blade_offset, owner)
    local_phase = ((theta % sector - table_offset) % sector).astype(jnp.int32)
    phase_sums = jnp.take(sector_sums, local_phase, axis=1)
    mean_fields = jnp.concatenate([phase_sums[0:1] / BLADES, phase_sums[1:4] / phase_sums[0:1], phase_sums[4:5] / BLADES], axis=0)
    fluctuation = velocity - mean_fields[1:4]
    taps = smoothing_taps(smooth_width)
    smoothed = jnp.zeros_like(fluctuation)
    for turn in range(2 * HW + 1):
        smoothed = smoothed + taps[turn] * jnp.roll(fluctuation, HW - turn, axis=1)
    dtheta = 2.0 * math.pi / AZ
    az_rate = (jnp.roll(smoothed, -1, axis=1) - jnp.roll(smoothed, 1, axis=1)) / (2.0 * dtheta)
    radial_rate = edge_rate(smoothed, 2)
    axial_rate = edge_rate(smoothed, 3)
    radius = (R / 2 + jnp.arange(R).astype(jnp.float32) + 0.5)[:, None]
    q_field = swirl_measure(smoothed, az_rate, radial_rate, axial_rate, radius)
    return mean_fields, q_field
```

```python
import math

import jax
import jax.numpy as jnp
from jax import lax
from jax.sharding import PartitionSpec as P

BLADES = 4
MAXOFF = 4
HW = 4
AZ = ("blade", "slab")


def passed_along(block, axis, distance):
    devices = range(lax.axis_size(axis))
    route = [((i - distance) % len(devices), i) for i in devices]
    return lax.ppermute(block, axis, route)


def extended(block, sides, width, periodic):
    for axis, dim in sides:
        count = lax.axis_size(axis)
        forward = [(i, i + 1) for i in range(count - 1)]
        if periodic:
            forward.append((count - 1, 0))
        backward = [(target, source) for source, target in forward]
        low = lax.ppermute(
            lax.slice_in_dim(block, block.shape[dim] - width, None, axis=dim), axis, forward
        )
        high = lax.ppermute(lax.slice_in_dim(block, 0, width, axis=dim), axis, backward)
        block = jnp.concatenate([low, block, high], axis=dim)
    return block


def smoothing_taps(smooth_width):
    spread = jnp.arange(-HW, HW + 1)
    width = smooth_width.astype(jnp.float32)
    square = (spread.astype(jnp.float32) ** 2)[:, None]
    weights = jnp.where(
        jnp.abs(spread)[:, None] <= smooth_width[None, :],
        jnp.exp(-0.5 * square / (width * width)[None, :]),
        0.0,
    )
    return weights / jnp.sum(weights, axis=0, keepdims=True)


def apply_taps(source, taps, length):
    total = jnp.zeros(source.shape[:1] + (length,) + source.shape[2:], jnp.float32)
    for turn in range(2 * HW + 1):
        total = total + taps[turn] * source[:, turn : turn + length]
    return total


def edge_rate(field, axis):
    count = field.shape[axis]
    upper = jnp.concatenate(
        [
            lax.slice_in_dim(field, 1, count, axis=axis),
            lax.slice_in_dim(field, count - 1, count, axis=axis),
        ],
        axis=axis,
    )
    lower = jnp.concatenate(
        [
            lax.slice_in_dim(field, 0, 1, axis=axis),
            lax.slice_in_dim(field, 0, count - 1, axis=axis),
        ],
        axis=axis,
    )
    places = jnp.arange(count)
    span = jnp.where((places == 0) | (places == count - 1), 1.0, 2.0).astype(field.dtype)
    layout = [1] * field.ndim
    layout[axis] = count
    return (upper - lower) / span.reshape(layout)


def swirl_measure(smoothed, az_rate, radial_rate, axial_rate, radius):
    tensor_aa = radial_rate[0]
    tensor_ab = (az_rate[0] - smoothed[1]) / radius
    tensor_ac = axial_rate[0]
    tensor_ba = radial_rate[1]
    tensor_bb = (az_rate[1] + smoothed[0]) / radius
    tensor_bc = axial_rate[1]
    tensor_ca = radial_rate[2]
    tensor_cb = az_rate[2] / radius
    tensor_cc = axial_rate[2]
    diagonal_part = tensor_aa * tensor_aa + tensor_bb * tensor_bb + tensor_cc * tensor_cc
    cross_part = tensor_ab * tensor_ba + tensor_ac * tensor_ca + tensor_bc * tensor_cb
    return -0.5 * (diagonal_part + 2.0 * cross_part)


def shards(density, flow_vars, blade_offset, smooth_width):
    cells = density.shape[0]
    rad_cells = density.shape[1]
    group = lax.axis_size("slab")
    blade = lax.axis_index("blade")
    own_offset = jnp.sum(jnp.where(jnp.arange(BLADES) == blade, blade_offset, 0))
    velocity = flow_vars[0:3]
    carried = jnp.concatenate([density[None], density[None] * velocity, flow_vars[3:4]], axis=0)
    ahead = passed_along(carried[:, :MAXOFF], AZ, -1)
    contribution = lax.dynamic_slice_in_dim(
        jnp.concatenate([carried, ahead], axis=1), own_offset, cells, 1
    )
    sector_part = lax.psum(contribution, "blade")
    behind = passed_along(sector_part[:, cells - MAXOFF :], AZ, 1)
    phase_sums = lax.dynamic_slice_in_dim(
        jnp.concatenate([behind, sector_part], axis=1), MAXOFF - own_offset, cells, 1
    )
    mean_fields = jnp.concatenate(
        [phase_sums[0:1] / BLADES, phase_sums[1:4] / phase_sums[0:1], phase_sums[4:5] / BLADES],
        axis=0,
    )
    fluctuation = velocity - mean_fields[1:4]
    taps = smoothing_taps(smooth_width)
    rimmed = extended(fluctuation, ((AZ, 1),), HW, True)
    smoothed = apply_taps(rimmed, taps, cells)
    az_side = extended(smoothed, ((AZ, 1),), 1, True)
    rad_side = extended(smoothed, (("rad", 2),), 1, False)
    dtheta = 2.0 * math.pi / (cells * lax.axis_size(AZ))
    az_rate = (az_side[:, 2:] - az_side[:, :-2]) / (2.0 * dtheta)
    total_rad = rad_cells * lax.axis_size("rad")
    rows = lax.axis_index("rad") * rad_cells + jnp.arange(rad_cells)
    upper = jnp.where((rows == total_rad - 1)[:, None], smoothed, rad_side[:, :, 2:])
    lower = jnp.where((rows == 0)[:, None], smoothed, rad_side[:, :, :-2])
    span = jnp.where((rows == 0) | (rows == total_rad - 1), 1.0, 2.0).astype(jnp.float32)
    radial_rate = (upper - lower) / span[:, None]
    axial_rate = edge_rate(smoothed, 3)
    radius = (total_rad / 2 + rows.astype(jnp.float32) + 0.5)[:, None]
    q_field = swirl_measure(smoothed, az_rate, radial_rate, axial_rate, radius)
    return (mean_fields, q_field)


def solution(mesh):
    az, rad = mesh.devices.shape
    split = jax.sharding.Mesh(mesh.devices.reshape(BLADES, az // BLADES, rad), ("blade", "slab", "rad"))
    in_specs = (P(AZ, "rad", None), P(None, AZ, "rad", None), P(), P())
    out_specs = (P(None, AZ, "rad", None), P(AZ, "rad", None))
    return jax.shard_map(shards, mesh=split, in_specs=in_specs, out_specs=out_specs, check_vma=False)
```

```python
import math

import jax
import jax.numpy as jnp
from jax import lax
from jax.sharding import PartitionSpec as P

BLADES = 4
MAXOFF = 4
HW = 4
AZ = ("blade", "slab")


def passed_along(block, axis, distance):
    devices = range(lax.axis_size(axis))
    route = [((i - distance) % len(devices), i) for i in devices]
    return lax.ppermute(block, axis, route)


def extended(block, sides, width, periodic):
    for axis, dim in sides:
        count = lax.axis_size(axis)
        forward = [(i, i + 1) for i in range(count - 1)]
        if periodic:
            forward.append((count - 1, 0))
        backward = [(target, source) for source, target in forward]
        low = lax.ppermute(
            lax.slice_in_dim(block, block.shape[dim] - width, None, axis=dim), axis, forward
        )
        high = lax.ppermute(lax.slice_in_dim(block, 0, width, axis=dim), axis, backward)
        block = jnp.concatenate([low, block, high], axis=dim)
    return block


def ring_half(block, step):
    count = lax.axis_size("blade")
    place = lax.axis_index("blade")
    route = [(i, (i + step) % count) for i in range(count)]
    width = block.shape[1] // count
    doubled = jnp.concatenate([block, block], axis=1)

    def piece(index):
        return lax.dynamic_slice_in_dim(doubled, index * width, width, 1)

    total = piece(place % count)
    for turn in range(1, count):
        total = lax.ppermute(total, "blade", route) + piece((place - step * turn) % count)
    pieces = [total]
    for turn in range(1, count):
        pieces.append(lax.ppermute(pieces[-1], "blade", route))
    if step > 0:
        sequence, first = pieces[::-1], (place - 2) % count
    else:
        sequence, first = pieces, (place - 1) % count
    ordered = jnp.concatenate(sequence * 2, axis=1)
    return lax.dynamic_slice_in_dim(ordered, ((count - first) % count) * width, block.shape[1], 1)


def ring_sum(block):
    half = block.shape[1] // 2
    return jnp.concatenate([ring_half(block[:, :half], 1), ring_half(block[:, half:], -1)], axis=1)


def smoothing_taps(smooth_width):
    spread = jnp.arange(-HW, HW + 1)
    width = smooth_width.astype(jnp.float32)
    square = (spread.astype(jnp.float32) ** 2)[:, None]
    weights = jnp.where(
        jnp.abs(spread)[:, None] <= smooth_width[None, :],
        jnp.exp(-0.5 * square / (width * width)[None, :]),
        0.0,
    )
    return weights / jnp.sum(weights, axis=0, keepdims=True)


def apply_taps(source, taps, length):
    total = jnp.zeros(source.shape[:1] + (length,) + source.shape[2:], jnp.float32)
    for turn in range(2 * HW + 1):
        total = total + taps[turn] * source[:, turn : turn + length]
    return total


def edge_rate(field, axis):
    count = field.shape[axis]
    upper = jnp.concatenate(
        [
            lax.slice_in_dim(field, 1, count, axis=axis),
            lax.slice_in_dim(field, count - 1, count, axis=axis),
        ],
        axis=axis,
    )
    lower = jnp.concatenate(
        [
            lax.slice_in_dim(field, 0, 1, axis=axis),
            lax.slice_in_dim(field, 0, count - 1, axis=axis),
        ],
        axis=axis,
    )
    places = jnp.arange(count)
    span = jnp.where((places == 0) | (places == count - 1), 1.0, 2.0).astype(field.dtype)
    layout = [1] * field.ndim
    layout[axis] = count
    return (upper - lower) / span.reshape(layout)


def swirl_measure(smoothed, az_rate, radial_rate, axial_rate, radius):
    tensor_aa = radial_rate[0]
    tensor_ab = (az_rate[0] - smoothed[1]) / radius
    tensor_ac = axial_rate[0]
    tensor_ba = radial_rate[1]
    tensor_bb = (az_rate[1] + smoothed[0]) / radius
    tensor_bc = axial_rate[1]
    tensor_ca = radial_rate[2]
    tensor_cb = az_rate[2] / radius
    tensor_cc = axial_rate[2]
    diagonal_part = tensor_aa * tensor_aa + tensor_bb * tensor_bb + tensor_cc * tensor_cc
    cross_part = tensor_ab * tensor_ba + tensor_ac * tensor_ca + tensor_bc * tensor_cb
    return -0.5 * (diagonal_part + 2.0 * cross_part)


def shards(density, flow_vars, blade_offset, smooth_width):
    cells = density.shape[0]
    rad_cells = density.shape[1]
    group = lax.axis_size("slab")
    blade = lax.axis_index("blade")
    own_offset = jnp.sum(jnp.where(jnp.arange(BLADES) == blade, blade_offset, 0))
    velocity = flow_vars[0:3]
    carried = jnp.concatenate([density[None], density[None] * velocity, flow_vars[3:4]], axis=0)
    ahead = passed_along(carried[:, :MAXOFF], AZ, -1)
    contribution = lax.dynamic_slice_in_dim(
        jnp.concatenate([carried, ahead], axis=1), own_offset, cells, 1
    )
    sector_part = ring_sum(contribution)
    behind = passed_along(sector_part[:, cells - MAXOFF :], AZ, 1)
    phase_sums = lax.dynamic_slice_in_dim(
        jnp.concatenate([behind, sector_part], axis=1), MAXOFF - own_offset, cells, 1
    )
    mean_fields = jnp.concatenate(
        [phase_sums[0:1] / BLADES, phase_sums[1:4] / phase_sums[0:1], phase_sums[4:5] / BLADES],
        axis=0,
    )
    fluctuation = velocity - mean_fields[1:4]
    taps = smoothing_taps(smooth_width)
    rimmed = extended(fluctuation, ((AZ, 1),), HW, True)
    smoothed = apply_taps(rimmed, taps, cells)
    az_side = extended(smoothed, ((AZ, 1),), 1, True)
    rad_side = extended(smoothed, (("rad", 2),), 1, False)
    dtheta = 2.0 * math.pi / (cells * lax.axis_size(AZ))
    az_rate = (az_side[:, 2:] - az_side[:, :-2]) / (2.0 * dtheta)
    total_rad = rad_cells * lax.axis_size("rad")
    rows = lax.axis_index("rad") * rad_cells + jnp.arange(rad_cells)
    upper = jnp.where((rows == total_rad - 1)[:, None], smoothed, rad_side[:, :, 2:])
    lower = jnp.where((rows == 0)[:, None], smoothed, rad_side[:, :, :-2])
    span = jnp.where((rows == 0) | (rows == total_rad - 1), 1.0, 2.0).astype(jnp.float32)
    radial_rate = (upper - lower) / span[:, None]
    axial_rate = edge_rate(smoothed, 3)
    radius = (total_rad / 2 + rows.astype(jnp.float32) + 0.5)[:, None]
    q_field = swirl_measure(smoothed, az_rate, radial_rate, axial_rate, radius)
    return (mean_fields, q_field)


def solution(mesh):
    az, rad = mesh.devices.shape
    split = jax.sharding.Mesh(mesh.devices.reshape(BLADES, az // BLADES, rad), ("blade", "slab", "rad"))
    in_specs = (P(AZ, "rad", None), P(None, AZ, "rad", None), P(), P())
    out_specs = (P(None, AZ, "rad", None), P(AZ, "rad", None))
    return jax.shard_map(shards, mesh=split, in_specs=in_specs, out_specs=out_specs, check_vma=False)
```

```python
import math

import jax
import jax.numpy as jnp
from jax import lax
from jax.sharding import PartitionSpec as P

BLADES = 4
MAXOFF = 4
HW = 4
AZ = ("blade", "slab")


def passed_along(block, axis, distance):
    devices = range(lax.axis_size(axis))
    route = [((i - distance) % len(devices), i) for i in devices]
    return lax.ppermute(block, axis, route)


def extended(block, sides, width, periodic):
    for axis, dim in sides:
        count = lax.axis_size(axis)
        forward = [(i, i + 1) for i in range(count - 1)]
        if periodic:
            forward.append((count - 1, 0))
        backward = [(target, source) for source, target in forward]
        low = lax.ppermute(
            lax.slice_in_dim(block, block.shape[dim] - width, None, axis=dim), axis, forward
        )
        high = lax.ppermute(lax.slice_in_dim(block, 0, width, axis=dim), axis, backward)
        block = jnp.concatenate([low, block, high], axis=dim)
    return block


def ring_half(block, step):
    count = lax.axis_size("blade")
    place = lax.axis_index("blade")
    route = [(i, (i + step) % count) for i in range(count)]
    width = block.shape[1] // count
    doubled = jnp.concatenate([block, block], axis=1)

    def piece(index):
        return lax.dynamic_slice_in_dim(doubled, index * width, width, 1)

    total = piece(place % count)
    for turn in range(1, count):
        total = lax.ppermute(total, "blade", route) + piece((place - step * turn) % count)
    pieces = [total]
    for turn in range(1, count):
        pieces.append(lax.ppermute(pieces[-1], "blade", route))
    if step > 0:
        sequence, first = pieces[::-1], (place - 2) % count
    else:
        sequence, first = pieces, (place - 1) % count
    ordered = jnp.concatenate(sequence * 2, axis=1)
    return lax.dynamic_slice_in_dim(ordered, ((count - first) % count) * width, block.shape[1], 1)


def ring_sum(block):
    half = block.shape[1] // 2
    return jnp.concatenate([ring_half(block[:, :half], 1), ring_half(block[:, half:], -1)], axis=1)


def smoothing_taps(smooth_width):
    spread = jnp.arange(-HW, HW + 1)
    width = smooth_width.astype(jnp.float32)
    square = (spread.astype(jnp.float32) ** 2)[:, None]
    weights = jnp.where(
        jnp.abs(spread)[:, None] <= smooth_width[None, :],
        jnp.exp(-0.5 * square / (width * width)[None, :]),
        0.0,
    )
    return weights / jnp.sum(weights, axis=0, keepdims=True)


def apply_taps(source, taps, length):
    total = jnp.zeros(source.shape[:1] + (length,) + source.shape[2:], jnp.float32)
    for turn in range(2 * HW + 1):
        total = total + taps[turn] * source[:, turn : turn + length]
    return total


def edge_rate(field, axis):
    count = field.shape[axis]
    upper = jnp.concatenate(
        [
            lax.slice_in_dim(field, 1, count, axis=axis),
            lax.slice_in_dim(field, count - 1, count, axis=axis),
        ],
        axis=axis,
    )
    lower = jnp.concatenate(
        [
            lax.slice_in_dim(field, 0, 1, axis=axis),
            lax.slice_in_dim(field, 0, count - 1, axis=axis),
        ],
        axis=axis,
    )
    places = jnp.arange(count)
    span = jnp.where((places == 0) | (places == count - 1), 1.0, 2.0).astype(field.dtype)
    layout = [1] * field.ndim
    layout[axis] = count
    return (upper - lower) / span.reshape(layout)


def swirl_measure(smoothed, az_rate, radial_rate, axial_rate, radius):
    tensor_aa = radial_rate[0]
    tensor_ab = (az_rate[0] - smoothed[1]) / radius
    tensor_ac = axial_rate[0]
    tensor_ba = radial_rate[1]
    tensor_bb = (az_rate[1] + smoothed[0]) / radius
    tensor_bc = axial_rate[1]
    tensor_ca = radial_rate[2]
    tensor_cb = az_rate[2] / radius
    tensor_cc = axial_rate[2]
    diagonal_part = tensor_aa * tensor_aa + tensor_bb * tensor_bb + tensor_cc * tensor_cc
    cross_part = tensor_ab * tensor_ba + tensor_ac * tensor_ca + tensor_bc * tensor_cb
    return -0.5 * (diagonal_part + 2.0 * cross_part)


def carry(raw):
    return jnp.concatenate([raw[0:1], raw[0:1] * raw[1:4], raw[4:5]], axis=0)


def shards(density, flow_vars, blade_offset, smooth_width):
    cells = density.shape[0]
    rad_cells = density.shape[1]
    group = lax.axis_size("slab")
    blade = lax.axis_index("blade")
    slab = lax.axis_index("slab")

    def offset_of(which):
        return jnp.sum(jnp.where(jnp.arange(BLADES) == which, blade_offset, 0))

    own_offset = offset_of(blade)
    prev_offset = offset_of(jnp.where(slab == 0, (blade + BLADES - 1) % BLADES, blade))
    next_offset = offset_of(jnp.where(slab == group - 1, (blade + 1) % BLADES, blade))
    reach = HW + 1
    velocity = flow_vars[0:3]
    raw = jnp.concatenate([density[None], flow_vars], axis=0)
    from_next = passed_along(raw[:, :reach], AZ, -1)
    from_prev = passed_along(velocity[:, cells - reach :], AZ, 1)
    carried = carry(raw)
    ahead = carry(from_next[:, :MAXOFF])
    contribution = lax.dynamic_slice_in_dim(
        jnp.concatenate([carried, ahead], axis=1), own_offset, cells, 1
    )
    sector_part = ring_sum(contribution)
    margin = MAXOFF + reach
    prev_part = passed_along(sector_part[:, cells - margin :], AZ, 1)
    next_part = passed_along(sector_part[:, :reach], AZ, -1)
    window = jnp.concatenate([prev_part, sector_part, next_part], axis=1)
    sums = jnp.concatenate(
        [
            lax.dynamic_slice_in_dim(window, MAXOFF - prev_offset, reach, 1),
            lax.dynamic_slice_in_dim(window, margin - own_offset, cells, 1),
            lax.dynamic_slice_in_dim(window, cells + margin - next_offset, reach, 1),
        ],
        axis=1,
    )
    means = jnp.concatenate(
        [sums[0:1] / BLADES, sums[1:4] / sums[0:1], sums[4:5] / BLADES], axis=0
    )
    mean_fields = means[:, reach : reach + cells]
    moving = jnp.concatenate([from_prev, velocity, from_next[1:4]], axis=1)
    fluctuation = moving - means[1:4]
    taps = smoothing_taps(smooth_width)
    rimmed = apply_taps(fluctuation, taps, cells + 2)
    smoothed = rimmed[:, 1 : cells + 1]
    rad_side = extended(smoothed, (("rad", 2),), 1, False)
    dtheta = 2.0 * math.pi / (cells * lax.axis_size(AZ))
    az_rate = (rimmed[:, 2:] - rimmed[:, :-2]) / (2.0 * dtheta)
    total_rad = rad_cells * lax.axis_size("rad")
    rows = lax.axis_index("rad") * rad_cells + jnp.arange(rad_cells)
    upper = jnp.where((rows == total_rad - 1)[:, None], smoothed, rad_side[:, :, 2:])
    lower = jnp.where((rows == 0)[:, None], smoothed, rad_side[:, :, :-2])
    span = jnp.where((rows == 0) | (rows == total_rad - 1), 1.0, 2.0).astype(jnp.float32)
    radial_rate = (upper - lower) / span[:, None]
    axial_rate = edge_rate(smoothed, 3)
    radius = (total_rad / 2 + rows.astype(jnp.float32) + 0.5)[:, None]
    q_field = swirl_measure(smoothed, az_rate, radial_rate, axial_rate, radius)
    return (mean_fields, q_field)


def solution(mesh):
    az, rad = mesh.devices.shape
    split = jax.sharding.Mesh(mesh.devices.reshape(BLADES, az // BLADES, rad), ("blade", "slab", "rad"))
    in_specs = (P(AZ, "rad", None), P(None, AZ, "rad", None), P(), P())
    out_specs = (P(None, AZ, "rad", None), P(AZ, "rad", None))
    return jax.shard_map(shards, mesh=split, in_specs=in_specs, out_specs=out_specs, check_vma=False)
```

```python
import math

import jax
import jax.numpy as jnp
from jax import lax
from jax.sharding import PartitionSpec as P

BLADES = 4
MAXOFF = 4
HW = 4
AZ = ("blade", "slab")


def passed_along(block, axis, distance):
    devices = range(lax.axis_size(axis))
    route = [((i - distance) % len(devices), i) for i in devices]
    return lax.ppermute(block, axis, route)


def extended(block, sides, width, periodic):
    for axis, dim in sides:
        count = lax.axis_size(axis)
        forward = [(i, i + 1) for i in range(count - 1)]
        if periodic:
            forward.append((count - 1, 0))
        backward = [(target, source) for source, target in forward]
        low = lax.ppermute(
            lax.slice_in_dim(block, block.shape[dim] - width, None, axis=dim), axis, forward
        )
        high = lax.ppermute(lax.slice_in_dim(block, 0, width, axis=dim), axis, backward)
        block = jnp.concatenate([low, block, high], axis=dim)
    return block


def ring_half(block, step):
    count = lax.axis_size("blade")
    place = lax.axis_index("blade")
    route = [(i, (i + step) % count) for i in range(count)]
    width = block.shape[1] // count
    doubled = jnp.concatenate([block, block], axis=1)

    def piece(index):
        return lax.dynamic_slice_in_dim(doubled, index * width, width, 1)

    total = piece(place % count)
    for turn in range(1, count):
        total = lax.ppermute(total, "blade", route) + piece((place - step * turn) % count)
    pieces = [total]
    for turn in range(1, count):
        pieces.append(lax.ppermute(pieces[-1], "blade", route))
    if step > 0:
        sequence, first = pieces[::-1], (place - 2) % count
    else:
        sequence, first = pieces, (place - 1) % count
    ordered = jnp.concatenate(sequence * 2, axis=1)
    return lax.dynamic_slice_in_dim(ordered, ((count - first) % count) * width, block.shape[1], 1)


def ring_sum(block):
    half = block.shape[1] // 2
    return jnp.concatenate([ring_half(block[:, :half], 1), ring_half(block[:, half:], -1)], axis=1)


def smoothing_taps(smooth_width):
    spread = jnp.arange(-HW, HW + 1)
    width = smooth_width.astype(jnp.float32)
    square = (spread.astype(jnp.float32) ** 2)[:, None]
    weights = jnp.where(
        jnp.abs(spread)[:, None] <= smooth_width[None, :],
        jnp.exp(-0.5 * square / (width * width)[None, :]),
        0.0,
    )
    return weights / jnp.sum(weights, axis=0, keepdims=True)


def apply_taps(source, taps, length):
    total = jnp.zeros(source.shape[:1] + (length,) + source.shape[2:], jnp.float32)
    for turn in range(2 * HW + 1):
        total = total + taps[turn] * source[:, turn : turn + length]
    return total


def edge_rate(field, axis):
    count = field.shape[axis]
    upper = jnp.concatenate(
        [
            lax.slice_in_dim(field, 1, count, axis=axis),
            lax.slice_in_dim(field, count - 1, count, axis=axis),
        ],
        axis=axis,
    )
    lower = jnp.concatenate(
        [
            lax.slice_in_dim(field, 0, 1, axis=axis),
            lax.slice_in_dim(field, 0, count - 1, axis=axis),
        ],
        axis=axis,
    )
    places = jnp.arange(count)
    span = jnp.where((places == 0) | (places == count - 1), 1.0, 2.0).astype(field.dtype)
    layout = [1] * field.ndim
    layout[axis] = count
    return (upper - lower) / span.reshape(layout)


def swirl_measure(smoothed, az_rate, radial_rate, axial_rate, radius):
    tensor_aa = radial_rate[0]
    tensor_ab = (az_rate[0] - smoothed[1]) / radius
    tensor_ac = axial_rate[0]
    tensor_ba = radial_rate[1]
    tensor_bb = (az_rate[1] + smoothed[0]) / radius
    tensor_bc = axial_rate[1]
    tensor_ca = radial_rate[2]
    tensor_cb = az_rate[2] / radius
    tensor_cc = axial_rate[2]
    diagonal_part = tensor_aa * tensor_aa + tensor_bb * tensor_bb + tensor_cc * tensor_cc
    cross_part = tensor_ab * tensor_ba + tensor_ac * tensor_ca + tensor_bc * tensor_cb
    return -0.5 * (diagonal_part + 2.0 * cross_part)


def carry(raw):
    return jnp.concatenate([raw[0:1], raw[0:1] * raw[1:4], raw[4:5]], axis=0)


def shards(density, flow_vars, blade_offset, smooth_width):
    cells = density.shape[0]
    rad_cells = density.shape[1]
    group = lax.axis_size("slab")
    blade = lax.axis_index("blade")
    slab = lax.axis_index("slab")

    def offset_of(which):
        return jnp.sum(jnp.where(jnp.arange(BLADES) == which, blade_offset, 0))

    own_offset = offset_of(blade)
    prev_offset = offset_of(jnp.where(slab == 0, (blade + BLADES - 1) % BLADES, blade))
    next_offset = offset_of(jnp.where(slab == group - 1, (blade + 1) % BLADES, blade))
    reach = HW + 1
    velocity = flow_vars[0:3]
    raw = jnp.concatenate([density[None], flow_vars], axis=0)
    from_next = passed_along(raw[:, :reach], AZ, -1)
    from_prev = passed_along(velocity[:, cells - reach :], AZ, 1)
    carried = carry(raw)
    ahead = carry(from_next[:, :MAXOFF])
    contribution = lax.dynamic_slice_in_dim(
        jnp.concatenate([carried, ahead], axis=1), own_offset, cells, 1
    )
    split = 3
    sector_part = jnp.concatenate(
        [lax.psum(contribution[:split], "blade"), ring_sum(contribution[split:])], axis=0
    )
    margin = MAXOFF + reach
    prev_part = passed_along(sector_part[:, cells - margin :], AZ, 1)
    next_part = passed_along(sector_part[:, :reach], AZ, -1)
    window = jnp.concatenate([prev_part, sector_part, next_part], axis=1)
    sums = jnp.concatenate(
        [
            lax.dynamic_slice_in_dim(window, MAXOFF - prev_offset, reach, 1),
            lax.dynamic_slice_in_dim(window, margin - own_offset, cells, 1),
            lax.dynamic_slice_in_dim(window, cells + margin - next_offset, reach, 1),
        ],
        axis=1,
    )
    means = jnp.concatenate(
        [sums[0:1] / BLADES, sums[1:4] / sums[0:1], sums[4:5] / BLADES], axis=0
    )
    mean_fields = means[:, reach : reach + cells]
    moving = jnp.concatenate([from_prev, velocity, from_next[1:4]], axis=1)
    fluctuation = moving - means[1:4]
    taps = smoothing_taps(smooth_width)
    rimmed = apply_taps(fluctuation, taps, cells + 2)
    smoothed = rimmed[:, 1 : cells + 1]
    rad_side = extended(smoothed, (("rad", 2),), 1, False)
    dtheta = 2.0 * math.pi / (cells * lax.axis_size(AZ))
    az_rate = (rimmed[:, 2:] - rimmed[:, :-2]) / (2.0 * dtheta)
    total_rad = rad_cells * lax.axis_size("rad")
    rows = lax.axis_index("rad") * rad_cells + jnp.arange(rad_cells)
    upper = jnp.where((rows == total_rad - 1)[:, None], smoothed, rad_side[:, :, 2:])
    lower = jnp.where((rows == 0)[:, None], smoothed, rad_side[:, :, :-2])
    span = jnp.where((rows == 0) | (rows == total_rad - 1), 1.0, 2.0).astype(jnp.float32)
    radial_rate = (upper - lower) / span[:, None]
    axial_rate = edge_rate(smoothed, 3)
    radius = (total_rad / 2 + rows.astype(jnp.float32) + 0.5)[:, None]
    q_field = swirl_measure(smoothed, az_rate, radial_rate, axial_rate, radius)
    return (mean_fields, q_field)


def solution(mesh):
    az, rad = mesh.devices.shape
    split = jax.sharding.Mesh(mesh.devices.reshape(BLADES, az // BLADES, rad), ("blade", "slab", "rad"))
    in_specs = (P(AZ, "rad", None), P(None, AZ, "rad", None), P(), P())
    out_specs = (P(None, AZ, "rad", None), P(AZ, "rad", None))
    return jax.shard_map(shards, mesh=split, in_specs=in_specs, out_specs=out_specs, check_vma=False)
```

```python
import math

import jax
import jax.numpy as jnp
from jax import lax
from jax.sharding import PartitionSpec as P

BLADES = 4
MAXOFF = 4
HW = 4
AZ = ("blade", "slab")


def passed_along(block, axis, distance):
    devices = range(lax.axis_size(axis))
    route = [((i - distance) % len(devices), i) for i in devices]
    return lax.ppermute(block, axis, route)


def extended(block, sides, width, periodic):
    for axis, dim in sides:
        count = lax.axis_size(axis)
        forward = [(i, i + 1) for i in range(count - 1)]
        if periodic:
            forward.append((count - 1, 0))
        backward = [(target, source) for source, target in forward]
        low = lax.ppermute(
            lax.slice_in_dim(block, block.shape[dim] - width, None, axis=dim), axis, forward
        )
        high = lax.ppermute(lax.slice_in_dim(block, 0, width, axis=dim), axis, backward)
        block = jnp.concatenate([low, block, high], axis=dim)
    return block


def ring_half(block, step):
    count = lax.axis_size("blade")
    place = lax.axis_index("blade")
    route = [(i, (i + step) % count) for i in range(count)]
    width = block.shape[1] // count
    doubled = jnp.concatenate([block, block], axis=1)

    def piece(index):
        return lax.dynamic_slice_in_dim(doubled, index * width, width, 1)

    total = piece(place % count)
    for turn in range(1, count):
        total = lax.ppermute(total, "blade", route) + piece((place - step * turn) % count)
    pieces = [total]
    for turn in range(1, count):
        pieces.append(lax.ppermute(pieces[-1], "blade", route))
    if step > 0:
        sequence, first = pieces[::-1], (place - 2) % count
    else:
        sequence, first = pieces, (place - 1) % count
    ordered = jnp.concatenate(sequence * 2, axis=1)
    return lax.dynamic_slice_in_dim(ordered, ((count - first) % count) * width, block.shape[1], 1)


def ring_sum(block):
    count = lax.axis_size("blade")
    half = block.shape[1] // 2
    parts = []
    for step, part in ((1, block[:, :half]), (-1, block[:, half:])):
        shape = part.shape
        if shape[1] % count:
            part = part.reshape(shape[0], shape[1] * 2, shape[2] // 2, shape[3])
        parts.append(ring_half(part, step).reshape(shape))
    return jnp.concatenate(parts, axis=1)


def smoothing_taps(smooth_width):
    spread = jnp.arange(-HW, HW + 1)
    width = smooth_width.astype(jnp.float32)
    square = (spread.astype(jnp.float32) ** 2)[:, None]
    weights = jnp.where(
        jnp.abs(spread)[:, None] <= smooth_width[None, :],
        jnp.exp(-0.5 * square / (width * width)[None, :]),
        0.0,
    )
    return weights / jnp.sum(weights, axis=0, keepdims=True)


def apply_taps(source, taps, length):
    total = jnp.zeros(source.shape[:1] + (length,) + source.shape[2:], jnp.float32)
    for turn in range(2 * HW + 1):
        total = total + taps[turn] * source[:, turn : turn + length]
    return total


def edge_rate(field, axis):
    count = field.shape[axis]
    upper = jnp.concatenate(
        [
            lax.slice_in_dim(field, 1, count, axis=axis),
            lax.slice_in_dim(field, count - 1, count, axis=axis),
        ],
        axis=axis,
    )
    lower = jnp.concatenate(
        [
            lax.slice_in_dim(field, 0, 1, axis=axis),
            lax.slice_in_dim(field, 0, count - 1, axis=axis),
        ],
        axis=axis,
    )
    places = jnp.arange(count)
    span = jnp.where((places == 0) | (places == count - 1), 1.0, 2.0).astype(field.dtype)
    layout = [1] * field.ndim
    layout[axis] = count
    return (upper - lower) / span.reshape(layout)


def swirl_measure(smoothed, az_rate, radial_rate, axial_rate, radius):
    tensor_aa = radial_rate[0]
    tensor_ab = (az_rate[0] - smoothed[1]) / radius
    tensor_ac = axial_rate[0]
    tensor_ba = radial_rate[1]
    tensor_bb = (az_rate[1] + smoothed[0]) / radius
    tensor_bc = axial_rate[1]
    tensor_ca = radial_rate[2]
    tensor_cb = az_rate[2] / radius
    tensor_cc = axial_rate[2]
    diagonal_part = tensor_aa * tensor_aa + tensor_bb * tensor_bb + tensor_cc * tensor_cc
    cross_part = tensor_ab * tensor_ba + tensor_ac * tensor_ca + tensor_bc * tensor_cb
    return -0.5 * (diagonal_part + 2.0 * cross_part)


def carry(raw):
    return jnp.concatenate([raw[0:1], raw[0:1] * raw[1:4], raw[4:5]], axis=0)


def shards(density, flow_vars, blade_offset, smooth_width):
    cells = density.shape[0]
    rad_cells = density.shape[1]
    group = lax.axis_size("slab")
    blade = lax.axis_index("blade")
    slab = lax.axis_index("slab")

    def offset_of(which):
        return jnp.sum(jnp.where(jnp.arange(BLADES) == which, blade_offset, 0))

    own_offset = offset_of(blade)
    prev_offset = offset_of(jnp.where(slab == 0, (blade + BLADES - 1) % BLADES, blade))
    next_offset = offset_of(jnp.where(slab == group - 1, (blade + 1) % BLADES, blade))
    reach = HW + 1
    velocity = flow_vars[0:3]
    raw = jnp.concatenate([density[None], flow_vars], axis=0)
    from_next = passed_along(raw[:, :reach], AZ, -1)
    from_prev = passed_along(velocity[:, cells - reach :], AZ, 1)
    carried = carry(raw)
    ahead = carry(from_next[:, :MAXOFF])
    early = lax.dynamic_slice_in_dim(carried, own_offset, cells - MAXOFF, 1)
    late = lax.dynamic_slice_in_dim(
        jnp.concatenate([carried[:, cells - MAXOFF :], ahead], axis=1), own_offset, MAXOFF, 1
    )
    sector_part = jnp.concatenate([lax.psum(early, "blade"), ring_sum(late)], axis=1)
    margin = MAXOFF + reach
    prev_part = passed_along(sector_part[:, cells - margin :], AZ, 1)
    next_part = passed_along(sector_part[:, :reach], AZ, -1)
    window = jnp.concatenate([prev_part, sector_part, next_part], axis=1)
    sums = jnp.concatenate(
        [
            lax.dynamic_slice_in_dim(window, MAXOFF - prev_offset, reach, 1),
            lax.dynamic_slice_in_dim(window, margin - own_offset, cells, 1),
            lax.dynamic_slice_in_dim(window, cells + margin - next_offset, reach, 1),
        ],
        axis=1,
    )
    means = jnp.concatenate(
        [sums[0:1] / BLADES, sums[1:4] / sums[0:1], sums[4:5] / BLADES], axis=0
    )
    mean_fields = means[:, reach : reach + cells]
    moving = jnp.concatenate([from_prev, velocity, from_next[1:4]], axis=1)
    fluctuation = moving - means[1:4]
    taps = smoothing_taps(smooth_width)
    rimmed = apply_taps(fluctuation, taps, cells + 2)
    smoothed = rimmed[:, 1 : cells + 1]
    rad_side = extended(smoothed, (("rad", 2),), 1, False)
    dtheta = 2.0 * math.pi / (cells * lax.axis_size(AZ))
    az_rate = (rimmed[:, 2:] - rimmed[:, :-2]) / (2.0 * dtheta)
    total_rad = rad_cells * lax.axis_size("rad")
    rows = lax.axis_index("rad") * rad_cells + jnp.arange(rad_cells)
    upper = jnp.where((rows == total_rad - 1)[:, None], smoothed, rad_side[:, :, 2:])
    lower = jnp.where((rows == 0)[:, None], smoothed, rad_side[:, :, :-2])
    span = jnp.where((rows == 0) | (rows == total_rad - 1), 1.0, 2.0).astype(jnp.float32)
    radial_rate = (upper - lower) / span[:, None]
    axial_rate = edge_rate(smoothed, 3)
    radius = (total_rad / 2 + rows.astype(jnp.float32) + 0.5)[:, None]
    q_field = swirl_measure(smoothed, az_rate, radial_rate, axial_rate, radius)
    return (mean_fields, q_field)


def solution(mesh):
    az, rad = mesh.devices.shape
    split = jax.sharding.Mesh(mesh.devices.reshape(BLADES, az // BLADES, rad), ("blade", "slab", "rad"))
    in_specs = (P(AZ, "rad", None), P(None, AZ, "rad", None), P(), P())
    out_specs = (P(None, AZ, "rad", None), P(AZ, "rad", None))
    return jax.shard_map(shards, mesh=split, in_specs=in_specs, out_specs=out_specs, check_vma=False)
```

```python
import math

import jax
import jax.numpy as jnp
from jax import lax
from jax.sharding import PartitionSpec as P

BLADES = 4
MAXOFF = 4
HW = 4
AZ = ("blade", "slab")


def passed_along(block, axis, distance):
    devices = range(lax.axis_size(axis))
    route = [((i - distance) % len(devices), i) for i in devices]
    return lax.ppermute(block, axis, route)


def extended(block, sides, width, periodic):
    for axis, dim in sides:
        count = lax.axis_size(axis)
        forward = [(i, i + 1) for i in range(count - 1)]
        if periodic:
            forward.append((count - 1, 0))
        backward = [(target, source) for source, target in forward]
        low = lax.ppermute(
            lax.slice_in_dim(block, block.shape[dim] - width, None, axis=dim), axis, forward
        )
        high = lax.ppermute(lax.slice_in_dim(block, 0, width, axis=dim), axis, backward)
        block = jnp.concatenate([low, block, high], axis=dim)
    return block


def ring_half(block, step):
    count = lax.axis_size("blade")
    place = lax.axis_index("blade")
    route = [(i, (i + step) % count) for i in range(count)]
    width = block.shape[1] // count
    doubled = jnp.concatenate([block, block], axis=1)

    def piece(index):
        return lax.dynamic_slice_in_dim(doubled, index * width, width, 1)

    total = piece(place % count)
    for turn in range(1, count):
        total = lax.ppermute(total, "blade", route) + piece((place - step * turn) % count)
    pieces = [total]
    for turn in range(1, count):
        pieces.append(lax.ppermute(pieces[-1], "blade", route))
    if step > 0:
        sequence, first = pieces[::-1], (place - 2) % count
    else:
        sequence, first = pieces, (place - 1) % count
    ordered = jnp.concatenate(sequence * 2, axis=1)
    return lax.dynamic_slice_in_dim(ordered, ((count - first) % count) * width, block.shape[1], 1)


def ring_sum(block):
    count = lax.axis_size("blade")
    half = block.shape[1] // 2
    parts = []
    for step, part in ((1, block[:, :half]), (-1, block[:, half:])):
        shape = part.shape
        if shape[1] % count:
            part = part.reshape(shape[0], shape[1] * 2, shape[2] // 2, shape[3])
        parts.append(ring_half(part, step).reshape(shape))
    return jnp.concatenate(parts, axis=1)


def smoothing_taps(smooth_width):
    spread = jnp.arange(-HW, HW + 1)
    width = smooth_width.astype(jnp.float32)
    square = (spread.astype(jnp.float32) ** 2)[:, None]
    weights = jnp.where(
        jnp.abs(spread)[:, None] <= smooth_width[None, :],
        jnp.exp(-0.5 * square / (width * width)[None, :]),
        0.0,
    )
    return weights / jnp.sum(weights, axis=0, keepdims=True)


def apply_taps(source, taps, length):
    total = jnp.zeros(source.shape[:1] + (length,) + source.shape[2:], jnp.float32)
    for turn in range(2 * HW + 1):
        total = total + taps[turn] * source[:, turn : turn + length]
    return total


def edge_rate(field, axis):
    count = field.shape[axis]
    upper = jnp.concatenate(
        [
            lax.slice_in_dim(field, 1, count, axis=axis),
            lax.slice_in_dim(field, count - 1, count, axis=axis),
        ],
        axis=axis,
    )
    lower = jnp.concatenate(
        [
            lax.slice_in_dim(field, 0, 1, axis=axis),
            lax.slice_in_dim(field, 0, count - 1, axis=axis),
        ],
        axis=axis,
    )
    places = jnp.arange(count)
    span = jnp.where((places == 0) | (places == count - 1), 1.0, 2.0).astype(field.dtype)
    layout = [1] * field.ndim
    layout[axis] = count
    return (upper - lower) / span.reshape(layout)


def swirl_measure(smoothed, az_rate, radial_rate, axial_rate, radius):
    tensor_aa = radial_rate[0]
    tensor_ab = (az_rate[0] - smoothed[1]) / radius
    tensor_ac = axial_rate[0]
    tensor_ba = radial_rate[1]
    tensor_bb = (az_rate[1] + smoothed[0]) / radius
    tensor_bc = axial_rate[1]
    tensor_ca = radial_rate[2]
    tensor_cb = az_rate[2] / radius
    tensor_cc = axial_rate[2]
    diagonal_part = tensor_aa * tensor_aa + tensor_bb * tensor_bb + tensor_cc * tensor_cc
    cross_part = tensor_ab * tensor_ba + tensor_ac * tensor_ca + tensor_bc * tensor_cb
    return -0.5 * (diagonal_part + 2.0 * cross_part)


def carry(raw):
    return jnp.concatenate([raw[0:1], raw[0:1] * raw[1:4], raw[4:5]], axis=0)


def shards(density, flow_vars, blade_offset, smooth_width):
    cells = density.shape[0]
    rad_cells = density.shape[1]
    group = lax.axis_size("slab")
    blade = lax.axis_index("blade")
    slab = lax.axis_index("slab")

    def offset_of(which):
        return jnp.sum(jnp.where(jnp.arange(BLADES) == which, blade_offset, 0))

    own_offset = offset_of(blade)
    prev_offset = offset_of(jnp.where(slab == 0, (blade + BLADES - 1) % BLADES, blade))
    next_offset = offset_of(jnp.where(slab == group - 1, (blade + 1) % BLADES, blade))
    reach = HW + 1
    velocity = flow_vars[0:3]
    raw = jnp.concatenate([density[None], flow_vars], axis=0)
    from_next = passed_along(raw[:, :reach], AZ, -1)
    from_prev = passed_along(velocity[:, cells - reach :], AZ, 1)
    carried = carry(raw)
    ahead = carry(from_next[:, :MAXOFF])
    early_cells = cells // 2
    early = lax.dynamic_slice_in_dim(carried, own_offset, early_cells, 1)
    late = lax.dynamic_slice_in_dim(
        jnp.concatenate([carried[:, early_cells:], ahead], axis=1),
        own_offset,
        cells - early_cells,
        1,
    )
    sector_part = jnp.concatenate([lax.psum(early, "blade"), ring_sum(late)], axis=1)
    margin = MAXOFF + reach
    prev_part = passed_along(sector_part[:, cells - margin :], AZ, 1)
    next_part = passed_along(sector_part[:, :reach], AZ, -1)
    window = jnp.concatenate([prev_part, sector_part, next_part], axis=1)
    sums = jnp.concatenate(
        [
            lax.dynamic_slice_in_dim(window, MAXOFF - prev_offset, reach, 1),
            lax.dynamic_slice_in_dim(window, margin - own_offset, cells, 1),
            lax.dynamic_slice_in_dim(window, cells + margin - next_offset, reach, 1),
        ],
        axis=1,
    )
    means = jnp.concatenate(
        [sums[0:1] / BLADES, sums[1:4] / sums[0:1], sums[4:5] / BLADES], axis=0
    )
    mean_fields = means[:, reach : reach + cells]
    moving = jnp.concatenate([from_prev, velocity, from_next[1:4]], axis=1)
    fluctuation = moving - means[1:4]
    taps = smoothing_taps(smooth_width)
    rimmed = apply_taps(fluctuation, taps, cells + 2)
    smoothed = rimmed[:, 1 : cells + 1]
    rad_side = extended(smoothed, (("rad", 2),), 1, False)
    dtheta = 2.0 * math.pi / (cells * lax.axis_size(AZ))
    az_rate = (rimmed[:, 2:] - rimmed[:, :-2]) / (2.0 * dtheta)
    total_rad = rad_cells * lax.axis_size("rad")
    rows = lax.axis_index("rad") * rad_cells + jnp.arange(rad_cells)
    upper = jnp.where((rows == total_rad - 1)[:, None], smoothed, rad_side[:, :, 2:])
    lower = jnp.where((rows == 0)[:, None], smoothed, rad_side[:, :, :-2])
    span = jnp.where((rows == 0) | (rows == total_rad - 1), 1.0, 2.0).astype(jnp.float32)
    radial_rate = (upper - lower) / span[:, None]
    axial_rate = edge_rate(smoothed, 3)
    radius = (total_rad / 2 + rows.astype(jnp.float32) + 0.5)[:, None]
    q_field = swirl_measure(smoothed, az_rate, radial_rate, axial_rate, radius)
    return (mean_fields, q_field)


def solution(mesh):
    az, rad = mesh.devices.shape
    split = jax.sharding.Mesh(mesh.devices.reshape(BLADES, az // BLADES, rad), ("blade", "slab", "rad"))
    in_specs = (P(AZ, "rad", None), P(None, AZ, "rad", None), P(), P())
    out_specs = (P(None, AZ, "rad", None), P(AZ, "rad", None))
    return jax.shard_map(shards, mesh=split, in_specs=in_specs, out_specs=out_specs, check_vma=False)
```

```python
import math

import jax
import jax.numpy as jnp
from jax import lax
from jax.sharding import PartitionSpec as P

BLADES = 4
MAXOFF = 4
HW = 4
AZ = ("blade", "slab")


def passed_along(block, axis, distance):
    devices = range(lax.axis_size(axis))
    route = [((i - distance) % len(devices), i) for i in devices]
    return lax.ppermute(block, axis, route)


def extended(block, sides, width, periodic):
    for axis, dim in sides:
        count = lax.axis_size(axis)
        forward = [(i, i + 1) for i in range(count - 1)]
        if periodic:
            forward.append((count - 1, 0))
        backward = [(target, source) for source, target in forward]
        low = lax.ppermute(
            lax.slice_in_dim(block, block.shape[dim] - width, None, axis=dim), axis, forward
        )
        high = lax.ppermute(lax.slice_in_dim(block, 0, width, axis=dim), axis, backward)
        block = jnp.concatenate([low, block, high], axis=dim)
    return block


def ring_half(block, step):
    count = lax.axis_size("blade")
    place = lax.axis_index("blade")
    route = [(i, (i + step) % count) for i in range(count)]
    width = block.shape[1] // count
    doubled = jnp.concatenate([block, block], axis=1)

    def piece(index):
        return lax.dynamic_slice_in_dim(doubled, index * width, width, 1)

    total = piece(place % count)
    for turn in range(1, count):
        total = lax.ppermute(total, "blade", route) + piece((place - step * turn) % count)
    pieces = [total]
    for turn in range(1, count):
        pieces.append(lax.ppermute(pieces[-1], "blade", route))
    if step > 0:
        sequence, first = pieces[::-1], (place - 2) % count
    else:
        sequence, first = pieces, (place - 1) % count
    ordered = jnp.concatenate(sequence * 2, axis=1)
    return lax.dynamic_slice_in_dim(ordered, ((count - first) % count) * width, block.shape[1], 1)


def ring_sum(block):
    count = lax.axis_size("blade")
    half = block.shape[1] // 2
    parts = []
    for step, part in ((1, block[:, :half]), (-1, block[:, half:])):
        shape = part.shape
        if shape[1] % count:
            part = part.reshape(shape[0], shape[1] * 2, shape[2] // 2, shape[3])
        parts.append(ring_half(part, step).reshape(shape))
    return jnp.concatenate(parts, axis=1)


def smoothing_taps(smooth_width):
    spread = jnp.arange(-HW, HW + 1)
    width = smooth_width.astype(jnp.float32)
    square = (spread.astype(jnp.float32) ** 2)[:, None]
    weights = jnp.where(
        jnp.abs(spread)[:, None] <= smooth_width[None, :],
        jnp.exp(-0.5 * square / (width * width)[None, :]),
        0.0,
    )
    return weights / jnp.sum(weights, axis=0, keepdims=True)


def apply_taps(source, taps, length):
    total = jnp.zeros(source.shape[:1] + (length,) + source.shape[2:], jnp.float32)
    for turn in range(2 * HW + 1):
        total = total + taps[turn] * source[:, turn : turn + length]
    return total


def edge_rate(field, axis):
    count = field.shape[axis]
    upper = jnp.concatenate(
        [
            lax.slice_in_dim(field, 1, count, axis=axis),
            lax.slice_in_dim(field, count - 1, count, axis=axis),
        ],
        axis=axis,
    )
    lower = jnp.concatenate(
        [
            lax.slice_in_dim(field, 0, 1, axis=axis),
            lax.slice_in_dim(field, 0, count - 1, axis=axis),
        ],
        axis=axis,
    )
    places = jnp.arange(count)
    span = jnp.where((places == 0) | (places == count - 1), 1.0, 2.0).astype(field.dtype)
    layout = [1] * field.ndim
    layout[axis] = count
    return (upper - lower) / span.reshape(layout)


def swirl_measure(smoothed, az_rate, radial_rate, axial_rate, radius):
    tensor_aa = radial_rate[0]
    tensor_ab = (az_rate[0] - smoothed[1]) / radius
    tensor_ac = axial_rate[0]
    tensor_ba = radial_rate[1]
    tensor_bb = (az_rate[1] + smoothed[0]) / radius
    tensor_bc = axial_rate[1]
    tensor_ca = radial_rate[2]
    tensor_cb = az_rate[2] / radius
    tensor_cc = axial_rate[2]
    diagonal_part = tensor_aa * tensor_aa + tensor_bb * tensor_bb + tensor_cc * tensor_cc
    cross_part = tensor_ab * tensor_ba + tensor_ac * tensor_ca + tensor_bc * tensor_cb
    return -0.5 * (diagonal_part + 2.0 * cross_part)


def carry(raw):
    return jnp.concatenate([raw[0:1], raw[0:1] * raw[1:4], raw[4:5]], axis=0)


def shards(density, flow_vars, blade_offset, smooth_width):
    cells = density.shape[0]
    rad_cells = density.shape[1]
    group = lax.axis_size("slab")
    blade = lax.axis_index("blade")
    slab = lax.axis_index("slab")

    def offset_of(which):
        return jnp.sum(jnp.where(jnp.arange(BLADES) == which, blade_offset, 0))

    own_offset = offset_of(blade)
    next_offset = offset_of(jnp.where(slab == group - 1, (blade + 1) % BLADES, blade))
    reach = HW + 1
    velocity = flow_vars[0:3]
    raw = jnp.concatenate([density[None], flow_vars], axis=0)
    from_next = passed_along(raw[:, :reach], AZ, -1)
    carried = carry(raw)
    ahead = carry(from_next[:, :MAXOFF])
    early = lax.dynamic_slice_in_dim(carried, own_offset, cells - MAXOFF, 1)
    late = lax.dynamic_slice_in_dim(
        jnp.concatenate([carried[:, cells - MAXOFF :], ahead], axis=1), own_offset, MAXOFF, 1
    )
    sector_part = jnp.concatenate([lax.psum(early, "blade"), ring_sum(late)], axis=1)
    tail_sums = lax.dynamic_slice_in_dim(sector_part, cells - reach - own_offset, reach, 1)
    tail_means = tail_sums[1:4] / tail_sums[0:1]
    tail_fluctuation = velocity[:, cells - reach :] - tail_means
    fields = sector_part.shape[0]
    sent = jnp.concatenate(
        [
            tail_fluctuation.reshape((-1,) + tail_fluctuation.shape[2:]),
            sector_part[:, cells - MAXOFF :].reshape((-1,) + sector_part.shape[2:]),
        ],
        axis=0,
    )
    got = passed_along(sent, AZ, 1)
    prev_fluctuation = got[: 3 * reach].reshape(tail_fluctuation.shape)
    behind = got[3 * reach :].reshape((fields, MAXOFF) + sector_part.shape[2:])
    next_part = passed_along(sector_part[0:4, :reach], AZ, -1)
    own_sums = lax.dynamic_slice_in_dim(
        jnp.concatenate([behind, sector_part], axis=1), MAXOFF - own_offset, cells, 1
    )
    mean_fields = jnp.concatenate(
        [own_sums[0:1] / BLADES, own_sums[1:4] / own_sums[0:1], own_sums[4:5] / BLADES], axis=0
    )
    head_sums = lax.dynamic_slice_in_dim(
        jnp.concatenate([sector_part[0:4, cells - MAXOFF :], next_part], axis=1),
        MAXOFF - next_offset,
        reach,
        1,
    )
    head_fluctuation = from_next[1:4] - head_sums[1:4] / head_sums[0:1]
    fluctuation = jnp.concatenate(
        [prev_fluctuation, velocity - mean_fields[1:4], head_fluctuation], axis=1
    )
    taps = smoothing_taps(smooth_width)
    rimmed = apply_taps(fluctuation, taps, cells + 2)
    smoothed = rimmed[:, 1 : cells + 1]
    rad_side = extended(smoothed, (("rad", 2),), 1, False)
    dtheta = 2.0 * math.pi / (cells * lax.axis_size(AZ))
    az_rate = (rimmed[:, 2:] - rimmed[:, :-2]) / (2.0 * dtheta)
    total_rad = rad_cells * lax.axis_size("rad")
    rows = lax.axis_index("rad") * rad_cells + jnp.arange(rad_cells)
    upper = jnp.where((rows == total_rad - 1)[:, None], smoothed, rad_side[:, :, 2:])
    lower = jnp.where((rows == 0)[:, None], smoothed, rad_side[:, :, :-2])
    span = jnp.where((rows == 0) | (rows == total_rad - 1), 1.0, 2.0).astype(jnp.float32)
    radial_rate = (upper - lower) / span[:, None]
    axial_rate = edge_rate(smoothed, 3)
    radius = (total_rad / 2 + rows.astype(jnp.float32) + 0.5)[:, None]
    q_field = swirl_measure(smoothed, az_rate, radial_rate, axial_rate, radius)
    return (mean_fields, q_field)


def solution(mesh):
    az, rad = mesh.devices.shape
    split = jax.sharding.Mesh(mesh.devices.reshape(BLADES, az // BLADES, rad), ("blade", "slab", "rad"))
    in_specs = (P(AZ, "rad", None), P(None, AZ, "rad", None), P(), P())
    out_specs = (P(None, AZ, "rad", None), P(AZ, "rad", None))
    return jax.shard_map(shards, mesh=split, in_specs=in_specs, out_specs=out_specs, check_vma=False)
```

```python
import math

import jax
import jax.numpy as jnp
from jax import lax
from jax.sharding import PartitionSpec as P

BLADES = 4
MAXOFF = 4
HW = 4
AZ = ("blade", "slab")


def passed_along(block, axis, distance):
    devices = range(lax.axis_size(axis))
    route = [((i - distance) % len(devices), i) for i in devices]
    return lax.ppermute(block, axis, route)


def extended(block, sides, width, periodic):
    for axis, dim in sides:
        count = lax.axis_size(axis)
        forward = [(i, i + 1) for i in range(count - 1)]
        if periodic:
            forward.append((count - 1, 0))
        backward = [(target, source) for source, target in forward]
        low = lax.ppermute(
            lax.slice_in_dim(block, block.shape[dim] - width, None, axis=dim), axis, forward
        )
        high = lax.ppermute(lax.slice_in_dim(block, 0, width, axis=dim), axis, backward)
        block = jnp.concatenate([low, block, high], axis=dim)
    return block


def ring_half(block, step):
    count = lax.axis_size("blade")
    place = lax.axis_index("blade")
    route = [(i, (i + step) % count) for i in range(count)]
    width = block.shape[1] // count
    doubled = jnp.concatenate([block, block], axis=1)

    def piece(index):
        return lax.dynamic_slice_in_dim(doubled, index * width, width, 1)

    total = piece(place % count)
    for turn in range(1, count):
        total = lax.ppermute(total, "blade", route) + piece((place - step * turn) % count)
    pieces = [total]
    for turn in range(1, count):
        pieces.append(lax.ppermute(pieces[-1], "blade", route))
    if step > 0:
        sequence, first = pieces[::-1], (place - 2) % count
    else:
        sequence, first = pieces, (place - 1) % count
    ordered = jnp.concatenate(sequence * 2, axis=1)
    return lax.dynamic_slice_in_dim(ordered, ((count - first) % count) * width, block.shape[1], 1)


def direct_sum(block):
    count = lax.axis_size("blade")
    place = lax.axis_index("blade")
    shape = block.shape
    if shape[1] % count:
        block = block.reshape(shape[0], shape[1] * 2, shape[2] // 2, shape[3])
    width = block.shape[1] // count
    doubled = jnp.concatenate([block, block], axis=1)

    def piece(index):
        return lax.dynamic_slice_in_dim(doubled, index * width, width, 1)

    def shifted(value, step):
        return lax.ppermute(value, "blade", [(i, (i + step) % count) for i in range(count)])

    total = piece(place)
    for step in range(1, count):
        total = total + shifted(piece((place + step) % count), step)
    got = [total] + [shifted(total, step) for step in range(1, count)]
    ordered = jnp.concatenate(got[::-1] * 2, axis=1)
    first = (count - (place + 1) % count) % count
    return lax.dynamic_slice_in_dim(ordered, first * width, block.shape[1], 1).reshape(shape)


def ring_sum(block):
    count = lax.axis_size("blade")
    half = block.shape[1] // 2
    parts = []
    for step, part in ((1, block[:, :half]), (-1, block[:, half:])):
        shape = part.shape
        if shape[1] % count:
            part = part.reshape(shape[0], shape[1] * 2, shape[2] // 2, shape[3])
        parts.append(ring_half(part, step).reshape(shape))
    return jnp.concatenate(parts, axis=1)


def smoothing_taps(smooth_width):
    spread = jnp.arange(-HW, HW + 1)
    width = smooth_width.astype(jnp.float32)
    square = (spread.astype(jnp.float32) ** 2)[:, None]
    weights = jnp.where(
        jnp.abs(spread)[:, None] <= smooth_width[None, :],
        jnp.exp(-0.5 * square / (width * width)[None, :]),
        0.0,
    )
    return weights / jnp.sum(weights, axis=0, keepdims=True)


def apply_taps(source, taps, length):
    total = jnp.zeros(source.shape[:1] + (length,) + source.shape[2:], jnp.float32)
    for turn in range(2 * HW + 1):
        total = total + taps[turn] * source[:, turn : turn + length]
    return total


def edge_rate(field, axis):
    count = field.shape[axis]
    upper = jnp.concatenate(
        [
            lax.slice_in_dim(field, 1, count, axis=axis),
            lax.slice_in_dim(field, count - 1, count, axis=axis),
        ],
        axis=axis,
    )
    lower = jnp.concatenate(
        [
            lax.slice_in_dim(field, 0, 1, axis=axis),
            lax.slice_in_dim(field, 0, count - 1, axis=axis),
        ],
        axis=axis,
    )
    places = jnp.arange(count)
    span = jnp.where((places == 0) | (places == count - 1), 1.0, 2.0).astype(field.dtype)
    layout = [1] * field.ndim
    layout[axis] = count
    return (upper - lower) / span.reshape(layout)


def swirl_measure(smoothed, az_rate, radial_rate, axial_rate, radius):
    tensor_aa = radial_rate[0]
    tensor_ab = (az_rate[0] - smoothed[1]) / radius
    tensor_ac = axial_rate[0]
    tensor_ba = radial_rate[1]
    tensor_bb = (az_rate[1] + smoothed[0]) / radius
    tensor_bc = axial_rate[1]
    tensor_ca = radial_rate[2]
    tensor_cb = az_rate[2] / radius
    tensor_cc = axial_rate[2]
    diagonal_part = tensor_aa * tensor_aa + tensor_bb * tensor_bb + tensor_cc * tensor_cc
    cross_part = tensor_ab * tensor_ba + tensor_ac * tensor_ca + tensor_bc * tensor_cb
    return -0.5 * (diagonal_part + 2.0 * cross_part)


def carry(raw):
    return jnp.concatenate([raw[0:1], raw[0:1] * raw[1:4], raw[4:5]], axis=0)


def shards(density, flow_vars, blade_offset, smooth_width):
    cells = density.shape[0]
    rad_cells = density.shape[1]
    group = lax.axis_size("slab")
    blade = lax.axis_index("blade")
    slab = lax.axis_index("slab")

    def offset_of(which):
        return jnp.sum(jnp.where(jnp.arange(BLADES) == which, blade_offset, 0))

    own_offset = offset_of(blade)
    next_offset = offset_of(jnp.where(slab == group - 1, (blade + 1) % BLADES, blade))
    reach = HW + 1
    velocity = flow_vars[0:3]
    raw = jnp.concatenate([density[None], flow_vars], axis=0)
    from_next = passed_along(raw[:, :reach], AZ, -1)
    carried = carry(raw)
    ahead = carry(from_next[:, :MAXOFF])
    early_cells = cells - MAXOFF - 2
    early = lax.dynamic_slice_in_dim(carried, own_offset, early_cells, 1)
    late = lax.dynamic_slice_in_dim(
        jnp.concatenate([carried[:, early_cells:], ahead], axis=1),
        own_offset,
        cells - early_cells,
        1,
    )
    sector_part = jnp.concatenate([lax.psum(early, "blade"), direct_sum(late)], axis=1)
    tail_sums = lax.dynamic_slice_in_dim(sector_part, cells - reach - own_offset, reach, 1)
    tail_means = tail_sums[1:4] / tail_sums[0:1]
    tail_fluctuation = velocity[:, cells - reach :] - tail_means
    fields = sector_part.shape[0]
    sent = jnp.concatenate(
        [
            tail_fluctuation.reshape((-1,) + tail_fluctuation.shape[2:]),
            sector_part[:, cells - MAXOFF :].reshape((-1,) + sector_part.shape[2:]),
        ],
        axis=0,
    )
    got = passed_along(sent, AZ, 1)
    prev_fluctuation = got[: 3 * reach].reshape(tail_fluctuation.shape)
    behind = got[3 * reach :].reshape((fields, MAXOFF) + sector_part.shape[2:])
    next_part = passed_along(sector_part[0:4, :reach], AZ, -1)
    own_sums = lax.dynamic_slice_in_dim(
        jnp.concatenate([behind, sector_part], axis=1), MAXOFF - own_offset, cells, 1
    )
    mean_fields = jnp.concatenate(
        [own_sums[0:1] / BLADES, own_sums[1:4] / own_sums[0:1], own_sums[4:5] / BLADES], axis=0
    )
    head_sums = lax.dynamic_slice_in_dim(
        jnp.concatenate([sector_part[0:4, cells - MAXOFF :], next_part], axis=1),
        MAXOFF - next_offset,
        reach,
        1,
    )
    head_fluctuation = from_next[1:4] - head_sums[1:4] / head_sums[0:1]
    fluctuation = jnp.concatenate(
        [prev_fluctuation, velocity - mean_fields[1:4], head_fluctuation], axis=1
    )
    taps = smoothing_taps(smooth_width)
    rimmed = apply_taps(fluctuation, taps, cells + 2)
    smoothed = rimmed[:, 1 : cells + 1]
    rad_side = extended(smoothed, (("rad", 2),), 1, False)
    dtheta = 2.0 * math.pi / (cells * lax.axis_size(AZ))
    az_rate = (rimmed[:, 2:] - rimmed[:, :-2]) / (2.0 * dtheta)
    total_rad = rad_cells * lax.axis_size("rad")
    rows = lax.axis_index("rad") * rad_cells + jnp.arange(rad_cells)
    upper = jnp.where((rows == total_rad - 1)[:, None], smoothed, rad_side[:, :, 2:])
    lower = jnp.where((rows == 0)[:, None], smoothed, rad_side[:, :, :-2])
    span = jnp.where((rows == 0) | (rows == total_rad - 1), 1.0, 2.0).astype(jnp.float32)
    radial_rate = (upper - lower) / span[:, None]
    axial_rate = edge_rate(smoothed, 3)
    radius = (total_rad / 2 + rows.astype(jnp.float32) + 0.5)[:, None]
    q_field = swirl_measure(smoothed, az_rate, radial_rate, axial_rate, radius)
    return (mean_fields, q_field)


def solution(mesh):
    az, rad = mesh.devices.shape
    split = jax.sharding.Mesh(mesh.devices.reshape(BLADES, az // BLADES, rad), ("blade", "slab", "rad"))
    in_specs = (P(AZ, "rad", None), P(None, AZ, "rad", None), P(), P())
    out_specs = (P(None, AZ, "rad", None), P(AZ, "rad", None))
    return jax.shard_map(shards, mesh=split, in_specs=in_specs, out_specs=out_specs, check_vma=False)
```

```python
import math

import jax
import jax.numpy as jnp
from jax import lax
from jax.sharding import PartitionSpec as P

BLADES = 4
MAXOFF = 4
HW = 4
AZ = ("blade", "slab")


def passed_along(block, axis, distance):
    devices = range(lax.axis_size(axis))
    route = [((i - distance) % len(devices), i) for i in devices]
    return lax.ppermute(block, axis, route)


def extended(block, sides, width, periodic):
    for axis, dim in sides:
        count = lax.axis_size(axis)
        forward = [(i, i + 1) for i in range(count - 1)]
        if periodic:
            forward.append((count - 1, 0))
        backward = [(target, source) for source, target in forward]
        low = lax.ppermute(
            lax.slice_in_dim(block, block.shape[dim] - width, None, axis=dim), axis, forward
        )
        high = lax.ppermute(lax.slice_in_dim(block, 0, width, axis=dim), axis, backward)
        block = jnp.concatenate([low, block, high], axis=dim)
    return block


def ring_half(block, step):
    count = lax.axis_size("blade")
    place = lax.axis_index("blade")
    route = [(i, (i + step) % count) for i in range(count)]
    width = block.shape[1] // count
    doubled = jnp.concatenate([block, block], axis=1)

    def piece(index):
        return lax.dynamic_slice_in_dim(doubled, index * width, width, 1)

    total = piece(place % count)
    for turn in range(1, count):
        total = lax.ppermute(total, "blade", route) + piece((place - step * turn) % count)
    pieces = [total]
    for turn in range(1, count):
        pieces.append(lax.ppermute(pieces[-1], "blade", route))
    if step > 0:
        sequence, first = pieces[::-1], (place - 2) % count
    else:
        sequence, first = pieces, (place - 1) % count
    ordered = jnp.concatenate(sequence * 2, axis=1)
    return lax.dynamic_slice_in_dim(ordered, ((count - first) % count) * width, block.shape[1], 1)


def ring_sum(block):
    count = lax.axis_size("blade")
    half = block.shape[1] // 2
    parts = []
    for step, part in ((1, block[:, :half]), (-1, block[:, half:])):
        shape = part.shape
        if shape[1] % count:
            part = part.reshape(shape[0], shape[1] * 2, shape[2] // 2, shape[3])
        parts.append(ring_half(part, step).reshape(shape))
    return jnp.concatenate(parts, axis=1)


def rad_rim(block):
    count = lax.axis_size("rad")
    forward = [(i, i + 1) for i in range(count - 1)]
    backward = [(target, source) for source, target in forward]
    rows = block.shape[2]
    low = lax.ppermute(block[:, :, rows - 1], "rad", forward)
    high = lax.ppermute(block[:, :, 0], "rad", backward)
    return jnp.concatenate([low[:, :, None], block, high[:, :, None]], axis=2)


def smoothing_taps(smooth_width):
    spread = jnp.arange(-HW, HW + 1)
    width = smooth_width.astype(jnp.float32)
    square = (spread.astype(jnp.float32) ** 2)[:, None]
    weights = jnp.where(
        jnp.abs(spread)[:, None] <= smooth_width[None, :],
        jnp.exp(-0.5 * square / (width * width)[None, :]),
        0.0,
    )
    return weights / jnp.sum(weights, axis=0, keepdims=True)


def apply_taps(source, taps, length):
    total = jnp.zeros(source.shape[:1] + (length,) + source.shape[2:], jnp.float32)
    for turn in range(2 * HW + 1):
        total = total + taps[turn] * source[:, turn : turn + length]
    return total


def edge_rate(field, axis):
    count = field.shape[axis]
    upper = jnp.concatenate(
        [
            lax.slice_in_dim(field, 1, count, axis=axis),
            lax.slice_in_dim(field, count - 1, count, axis=axis),
        ],
        axis=axis,
    )
    lower = jnp.concatenate(
        [
            lax.slice_in_dim(field, 0, 1, axis=axis),
            lax.slice_in_dim(field, 0, count - 1, axis=axis),
        ],
        axis=axis,
    )
    places = jnp.arange(count)
    span = jnp.where((places == 0) | (places == count - 1), 1.0, 2.0).astype(field.dtype)
    layout = [1] * field.ndim
    layout[axis] = count
    return (upper - lower) / span.reshape(layout)


def swirl_measure(smoothed, az_rate, radial_rate, axial_rate, radius):
    tensor_aa = radial_rate[0]
    tensor_ab = (az_rate[0] - smoothed[1]) / radius
    tensor_ac = axial_rate[0]
    tensor_ba = radial_rate[1]
    tensor_bb = (az_rate[1] + smoothed[0]) / radius
    tensor_bc = axial_rate[1]
    tensor_ca = radial_rate[2]
    tensor_cb = az_rate[2] / radius
    tensor_cc = axial_rate[2]
    diagonal_part = tensor_aa * tensor_aa + tensor_bb * tensor_bb + tensor_cc * tensor_cc
    cross_part = tensor_ab * tensor_ba + tensor_ac * tensor_ca + tensor_bc * tensor_cb
    return -0.5 * (diagonal_part + 2.0 * cross_part)


def carry(raw):
    return jnp.concatenate([raw[0:1], raw[0:1] * raw[1:4], raw[4:5]], axis=0)


def shards(density, flow_vars, blade_offset, smooth_width):
    cells = density.shape[0]
    rad_cells = density.shape[1]
    group = lax.axis_size("slab")
    blade = lax.axis_index("blade")
    slab = lax.axis_index("slab")

    def offset_of(which):
        return jnp.sum(jnp.where(jnp.arange(BLADES) == which, blade_offset, 0))

    own_offset = offset_of(blade)
    next_offset = offset_of(jnp.where(slab == group - 1, (blade + 1) % BLADES, blade))
    reach = HW + 1
    velocity = flow_vars[0:3]
    raw = jnp.concatenate([density[None], flow_vars], axis=0)
    from_next = passed_along(raw[:, :reach], AZ, -1)
    carried = carry(raw)
    ahead = carry(from_next[:, :MAXOFF])
    early = carry(lax.dynamic_slice_in_dim(raw, own_offset, cells - MAXOFF, 1))
    late = lax.dynamic_slice_in_dim(
        jnp.concatenate([carried[:, cells - MAXOFF :], ahead], axis=1), own_offset, MAXOFF, 1
    )
    sector_part = jnp.concatenate([lax.psum(early, "blade"), ring_sum(late)], axis=1)
    tail_sums = lax.dynamic_slice_in_dim(sector_part, cells - reach - own_offset, reach, 1)
    tail_means = tail_sums[1:4] / tail_sums[0:1]
    tail_fluctuation = velocity[:, cells - reach :] - tail_means
    fields = sector_part.shape[0]
    sent = jnp.concatenate(
        [
            tail_fluctuation.reshape((-1,) + tail_fluctuation.shape[2:]),
            sector_part[:, cells - MAXOFF :].reshape((-1,) + sector_part.shape[2:]),
        ],
        axis=0,
    )
    got = passed_along(sent, AZ, 1)
    prev_fluctuation = got[: 3 * reach].reshape(tail_fluctuation.shape)
    behind = got[3 * reach :].reshape((fields, MAXOFF) + sector_part.shape[2:])
    next_part = passed_along(sector_part[0:4, :reach], AZ, -1)
    own_sums = lax.dynamic_slice_in_dim(
        jnp.concatenate([behind, sector_part], axis=1), MAXOFF - own_offset, cells, 1
    )
    mean_fields = jnp.concatenate(
        [own_sums[0:1] / BLADES, own_sums[1:4] / own_sums[0:1], own_sums[4:5] / BLADES], axis=0
    )
    head_sums = lax.dynamic_slice_in_dim(
        jnp.concatenate([sector_part[0:4, cells - MAXOFF :], next_part], axis=1),
        MAXOFF - next_offset,
        reach,
        1,
    )
    head_fluctuation = from_next[1:4] - head_sums[1:4] / head_sums[0:1]
    fluctuation = jnp.concatenate(
        [prev_fluctuation, velocity - mean_fields[1:4], head_fluctuation], axis=1
    )
    taps = smoothing_taps(smooth_width)
    rimmed = apply_taps(fluctuation, taps, cells + 2)
    smoothed = rimmed[:, 1 : cells + 1]
    rad_side = rad_rim(smoothed)
    dtheta = 2.0 * math.pi / (cells * lax.axis_size(AZ))
    az_rate = (rimmed[:, 2:] - rimmed[:, :-2]) / (2.0 * dtheta)
    total_rad = rad_cells * lax.axis_size("rad")
    rows = lax.axis_index("rad") * rad_cells + jnp.arange(rad_cells)
    upper = jnp.where((rows == total_rad - 1)[:, None], smoothed, rad_side[:, :, 2:])
    lower = jnp.where((rows == 0)[:, None], smoothed, rad_side[:, :, :-2])
    span = jnp.where((rows == 0) | (rows == total_rad - 1), 1.0, 2.0).astype(jnp.float32)
    radial_rate = (upper - lower) / span[:, None]
    axial_rate = edge_rate(smoothed, 3)
    radius = (total_rad / 2 + rows.astype(jnp.float32) + 0.5)[:, None]
    q_field = swirl_measure(smoothed, az_rate, radial_rate, axial_rate, radius)
    return (mean_fields, q_field)


def solution(mesh):
    az, rad = mesh.devices.shape
    split = jax.sharding.Mesh(mesh.devices.reshape(BLADES, az // BLADES, rad), ("blade", "slab", "rad"))
    in_specs = (P(AZ, "rad", None), P(None, AZ, "rad", None), P(), P())
    out_specs = (P(None, AZ, "rad", None), P(AZ, "rad", None))
    return jax.shard_map(shards, mesh=split, in_specs=in_specs, out_specs=out_specs, check_vma=False)
```

```python
import math

import jax
import jax.numpy as jnp
from jax import lax
from jax.sharding import PartitionSpec as P

BLADES = 4
MAXOFF = 4
HW = 4
AZ = ("blade", "slab")


def passed_along(block, axis, distance):
    devices = range(lax.axis_size(axis))
    route = [((i - distance) % len(devices), i) for i in devices]
    return lax.ppermute(block, axis, route)


def extended(block, sides, width, periodic):
    for axis, dim in sides:
        count = lax.axis_size(axis)
        forward = [(i, i + 1) for i in range(count - 1)]
        if periodic:
            forward.append((count - 1, 0))
        backward = [(target, source) for source, target in forward]
        low = lax.ppermute(
            lax.slice_in_dim(block, block.shape[dim] - width, None, axis=dim), axis, forward
        )
        high = lax.ppermute(lax.slice_in_dim(block, 0, width, axis=dim), axis, backward)
        block = jnp.concatenate([low, block, high], axis=dim)
    return block


def ring_half(block, step):
    count = lax.axis_size("blade")
    place = lax.axis_index("blade")
    route = [(i, (i + step) % count) for i in range(count)]
    width = block.shape[1] // count
    doubled = jnp.concatenate([block, block], axis=1)

    def piece(index):
        return lax.dynamic_slice_in_dim(doubled, index * width, width, 1)

    total = piece(place % count)
    for turn in range(1, count):
        total = lax.ppermute(total, "blade", route) + piece((place - step * turn) % count)
    pieces = [total]
    for turn in range(1, count):
        pieces.append(lax.ppermute(pieces[-1], "blade", route))
    if step > 0:
        sequence, first = pieces[::-1], (place - 2) % count
    else:
        sequence, first = pieces, (place - 1) % count
    ordered = jnp.concatenate(sequence * 2, axis=1)
    return lax.dynamic_slice_in_dim(ordered, ((count - first) % count) * width, block.shape[1], 1)


def ring_sum(block):
    count = lax.axis_size("blade")
    half = block.shape[1] // 2
    parts = []
    for step, part in ((1, block[:, :half]), (-1, block[:, half:])):
        shape = part.shape
        if shape[1] % count:
            part = part.reshape(shape[0], shape[1] * 2, shape[2] // 2, shape[3])
        parts.append(ring_half(part, step).reshape(shape))
    return jnp.concatenate(parts, axis=1)


def rad_rim(block, edges, taps, cells):
    count = lax.axis_size("rad")
    forward = [(i, i + 1) for i in range(count - 1)]
    backward = [(target, source) for source, target in forward]
    edge_rows = apply_taps(edges, taps, cells + 2)[:, 1 : cells + 1]
    low = lax.ppermute(edge_rows[:, :, 1], "rad", forward)
    high = lax.ppermute(edge_rows[:, :, 0], "rad", backward)
    return jnp.concatenate([low[:, :, None], block, high[:, :, None]], axis=2)


def smoothing_taps(smooth_width):
    spread = jnp.arange(-HW, HW + 1)
    width = smooth_width.astype(jnp.float32)
    square = (spread.astype(jnp.float32) ** 2)[:, None]
    weights = jnp.where(
        jnp.abs(spread)[:, None] <= smooth_width[None, :],
        jnp.exp(-0.5 * square / (width * width)[None, :]),
        0.0,
    )
    return weights / jnp.sum(weights, axis=0, keepdims=True)


def apply_taps(source, taps, length):
    total = jnp.zeros(source.shape[:1] + (length,) + source.shape[2:], jnp.float32)
    for turn in range(2 * HW + 1):
        total = total + taps[turn] * source[:, turn : turn + length]
    return total


def edge_rate(field, axis):
    count = field.shape[axis]
    upper = jnp.concatenate(
        [
            lax.slice_in_dim(field, 1, count, axis=axis),
            lax.slice_in_dim(field, count - 1, count, axis=axis),
        ],
        axis=axis,
    )
    lower = jnp.concatenate(
        [
            lax.slice_in_dim(field, 0, 1, axis=axis),
            lax.slice_in_dim(field, 0, count - 1, axis=axis),
        ],
        axis=axis,
    )
    places = jnp.arange(count)
    span = jnp.where((places == 0) | (places == count - 1), 1.0, 2.0).astype(field.dtype)
    layout = [1] * field.ndim
    layout[axis] = count
    return (upper - lower) / span.reshape(layout)


def swirl_measure(smoothed, az_rate, radial_rate, axial_rate, radius):
    tensor_aa = radial_rate[0]
    tensor_ab = (az_rate[0] - smoothed[1]) / radius
    tensor_ac = axial_rate[0]
    tensor_ba = radial_rate[1]
    tensor_bb = (az_rate[1] + smoothed[0]) / radius
    tensor_bc = axial_rate[1]
    tensor_ca = radial_rate[2]
    tensor_cb = az_rate[2] / radius
    tensor_cc = axial_rate[2]
    diagonal_part = tensor_aa * tensor_aa + tensor_bb * tensor_bb + tensor_cc * tensor_cc
    cross_part = tensor_ab * tensor_ba + tensor_ac * tensor_ca + tensor_bc * tensor_cb
    return -0.5 * (diagonal_part + 2.0 * cross_part)


def carry(raw):
    return jnp.concatenate([raw[0:1], raw[0:1] * raw[1:4], raw[4:5]], axis=0)


def shards(density, flow_vars, blade_offset, smooth_width):
    cells = density.shape[0]
    rad_cells = density.shape[1]
    group = lax.axis_size("slab")
    blade = lax.axis_index("blade")
    slab = lax.axis_index("slab")

    def offset_of(which):
        return jnp.sum(jnp.where(jnp.arange(BLADES) == which, blade_offset, 0))

    own_offset = offset_of(blade)
    next_offset = offset_of(jnp.where(slab == group - 1, (blade + 1) % BLADES, blade))
    reach = HW + 1
    velocity = flow_vars[0:3]
    raw = jnp.concatenate([density[None], flow_vars], axis=0)
    from_next = passed_along(raw[:, :reach], AZ, -1)
    carried = carry(raw)
    ahead = carry(from_next[:, :MAXOFF])
    early = carry(lax.dynamic_slice_in_dim(raw, own_offset, cells - MAXOFF, 1))
    late = lax.dynamic_slice_in_dim(
        jnp.concatenate([carried[:, cells - MAXOFF :], ahead], axis=1), own_offset, MAXOFF, 1
    )
    early_sums = lax.psum(early, "blade")
    late_sums = ring_sum(late)
    sector_part = jnp.concatenate([early_sums, late_sums], axis=1)
    last = jnp.concatenate([early_sums[:, cells - MAXOFF - reach :], late_sums], axis=1)
    tail_sums = lax.dynamic_slice_in_dim(last, MAXOFF - own_offset, reach, 1)
    tail_means = tail_sums[1:4] / tail_sums[0:1]
    tail_fluctuation = velocity[:, cells - reach :] - tail_means
    fields = sector_part.shape[0]
    sent = jnp.concatenate(
        [
            tail_fluctuation.reshape((-1,) + tail_fluctuation.shape[2:]),
            late_sums.reshape((-1,) + sector_part.shape[2:]),
        ],
        axis=0,
    )
    got = passed_along(sent, AZ, 1)
    prev_fluctuation = got[: 3 * reach].reshape(tail_fluctuation.shape)
    behind = got[3 * reach :].reshape((fields, MAXOFF) + sector_part.shape[2:])
    next_part = passed_along(early_sums[0:4, :reach], AZ, -1)
    own_sums = lax.dynamic_slice_in_dim(
        jnp.concatenate([behind, sector_part], axis=1), MAXOFF - own_offset, cells, 1
    )
    mean_fields = jnp.concatenate(
        [own_sums[0:1] / BLADES, own_sums[1:4] / own_sums[0:1], own_sums[4:5] / BLADES], axis=0
    )
    head_sums = lax.dynamic_slice_in_dim(
        jnp.concatenate([late_sums[0:4], next_part], axis=1),
        MAXOFF - next_offset,
        reach,
        1,
    )
    head_fluctuation = from_next[1:4] - head_sums[1:4] / head_sums[0:1]
    fluctuation = jnp.concatenate(
        [prev_fluctuation, velocity - mean_fields[1:4], head_fluctuation], axis=1
    )
    taps = smoothing_taps(smooth_width)
    rimmed = apply_taps(fluctuation, taps, cells + 2)
    smoothed = rimmed[:, 1 : cells + 1]
    rad_side = rad_rim(
        smoothed,
        jnp.concatenate([fluctuation[:, :, :1], fluctuation[:, :, -1:]], axis=2),
        taps,
        cells,
    )
    dtheta = 2.0 * math.pi / (cells * lax.axis_size(AZ))
    az_rate = (rimmed[:, 2:] - rimmed[:, :-2]) / (2.0 * dtheta)
    total_rad = rad_cells * lax.axis_size("rad")
    rows = lax.axis_index("rad") * rad_cells + jnp.arange(rad_cells)
    upper = jnp.where((rows == total_rad - 1)[:, None], smoothed, rad_side[:, :, 2:])
    lower = jnp.where((rows == 0)[:, None], smoothed, rad_side[:, :, :-2])
    span = jnp.where((rows == 0) | (rows == total_rad - 1), 1.0, 2.0).astype(jnp.float32)
    radial_rate = (upper - lower) / span[:, None]
    axial_rate = edge_rate(smoothed, 3)
    radius = (total_rad / 2 + rows.astype(jnp.float32) + 0.5)[:, None]
    q_field = swirl_measure(smoothed, az_rate, radial_rate, axial_rate, radius)
    return (mean_fields, q_field)


def solution(mesh):
    az, rad = mesh.devices.shape
    split = jax.sharding.Mesh(mesh.devices.reshape(BLADES, az // BLADES, rad), ("blade", "slab", "rad"))
    in_specs = (P(AZ, "rad", None), P(None, AZ, "rad", None), P(), P())
    out_specs = (P(None, AZ, "rad", None), P(AZ, "rad", None))
    return jax.shard_map(shards, mesh=split, in_specs=in_specs, out_specs=out_specs, check_vma=False)
```

```python
import math

import jax
import jax.numpy as jnp
from jax import lax
from jax.sharding import PartitionSpec as P

BLADES = 4
MAXOFF = 4
HW = 4
AZ = ("blade", "slab")


def passed_along(block, axis, distance):
    devices = range(lax.axis_size(axis))
    route = [((i - distance) % len(devices), i) for i in devices]
    return lax.ppermute(block, axis, route)


def extended(block, sides, width, periodic):
    for axis, dim in sides:
        count = lax.axis_size(axis)
        forward = [(i, i + 1) for i in range(count - 1)]
        if periodic:
            forward.append((count - 1, 0))
        backward = [(target, source) for source, target in forward]
        low = lax.ppermute(
            lax.slice_in_dim(block, block.shape[dim] - width, None, axis=dim), axis, forward
        )
        high = lax.ppermute(lax.slice_in_dim(block, 0, width, axis=dim), axis, backward)
        block = jnp.concatenate([low, block, high], axis=dim)
    return block


def ring_half(block, step):
    count = lax.axis_size("blade")
    place = lax.axis_index("blade")
    route = [(i, (i + step) % count) for i in range(count)]
    width = block.shape[1] // count
    doubled = jnp.concatenate([block, block], axis=1)

    def piece(index):
        return lax.dynamic_slice_in_dim(doubled, index * width, width, 1)

    total = piece(place % count)
    for turn in range(1, count):
        total = lax.ppermute(total, "blade", route) + piece((place - step * turn) % count)
    pieces = [total]
    for turn in range(1, count):
        pieces.append(lax.ppermute(pieces[-1], "blade", route))
    if step > 0:
        sequence, first = pieces[::-1], (place - 2) % count
    else:
        sequence, first = pieces, (place - 1) % count
    ordered = jnp.concatenate(sequence * 2, axis=1)
    return lax.dynamic_slice_in_dim(ordered, ((count - first) % count) * width, block.shape[1], 1)


def ring_sum(block):
    count = lax.axis_size("blade")
    half = block.shape[1] // 2
    parts = []
    for step, part in ((1, block[:, :half]), (-1, block[:, half:])):
        shape = part.shape
        if shape[1] % count:
            part = part.reshape(shape[0], shape[1] * 2, shape[2] // 2, shape[3])
        parts.append(ring_half(part, step).reshape(shape))
    return jnp.concatenate(parts, axis=1)


def rad_rim(block, edges, taps, cells):
    count = lax.axis_size("rad")
    forward = [(i, i + 1) for i in range(count - 1)]
    backward = [(target, source) for source, target in forward]
    edge_rows = apply_taps(edges, taps, cells + 2)[:, 1 : cells + 1]
    low = lax.ppermute(edge_rows[:, :, 1], "rad", forward)
    high = lax.ppermute(edge_rows[:, :, 0], "rad", backward)
    return jnp.concatenate([low[:, :, None], block, high[:, :, None]], axis=2)


def smoothing_taps(smooth_width):
    spread = jnp.arange(-HW, HW + 1)
    width = smooth_width.astype(jnp.float32)
    square = (spread.astype(jnp.float32) ** 2)[:, None]
    weights = jnp.where(
        jnp.abs(spread)[:, None] <= smooth_width[None, :],
        jnp.exp(-0.5 * square / (width * width)[None, :]),
        0.0,
    )
    return weights / jnp.sum(weights, axis=0, keepdims=True)


def apply_taps(source, taps, length):
    total = jnp.zeros(source.shape[:1] + (length,) + source.shape[2:], jnp.float32)
    for turn in range(2 * HW + 1):
        total = total + taps[turn] * source[:, turn : turn + length]
    return total


def edge_rate(field, axis):
    count = field.shape[axis]
    upper = jnp.concatenate(
        [
            lax.slice_in_dim(field, 1, count, axis=axis),
            lax.slice_in_dim(field, count - 1, count, axis=axis),
        ],
        axis=axis,
    )
    lower = jnp.concatenate(
        [
            lax.slice_in_dim(field, 0, 1, axis=axis),
            lax.slice_in_dim(field, 0, count - 1, axis=axis),
        ],
        axis=axis,
    )
    places = jnp.arange(count)
    span = jnp.where((places == 0) | (places == count - 1), 1.0, 2.0).astype(field.dtype)
    layout = [1] * field.ndim
    layout[axis] = count
    return (upper - lower) / span.reshape(layout)


def swirl_measure(smoothed, az_rate, radial_rate, axial_rate, radius):
    tensor_aa = radial_rate[0]
    tensor_ab = (az_rate[0] - smoothed[1]) / radius
    tensor_ac = axial_rate[0]
    tensor_ba = radial_rate[1]
    tensor_bb = (az_rate[1] + smoothed[0]) / radius
    tensor_bc = axial_rate[1]
    tensor_ca = radial_rate[2]
    tensor_cb = az_rate[2] / radius
    tensor_cc = axial_rate[2]
    diagonal_part = tensor_aa * tensor_aa + tensor_bb * tensor_bb + tensor_cc * tensor_cc
    cross_part = tensor_ab * tensor_ba + tensor_ac * tensor_ca + tensor_bc * tensor_cb
    return -0.5 * (diagonal_part + 2.0 * cross_part)


def carry(raw):
    return jnp.concatenate([raw[0:1], raw[0:1] * raw[1:4], raw[4:5]], axis=0)


def shards(density, flow_vars, blade_offset, smooth_width):
    cells = density.shape[0]
    rad_cells = density.shape[1]
    group = lax.axis_size("slab")
    blade = lax.axis_index("blade")
    slab = lax.axis_index("slab")

    def offset_of(which):
        return jnp.sum(jnp.where(jnp.arange(BLADES) == which, blade_offset, 0))

    own_offset = offset_of(blade)
    next_offset = offset_of(jnp.where(slab == group - 1, (blade + 1) % BLADES, blade))
    reach = HW + 1
    velocity = flow_vars[0:3]
    raw = jnp.concatenate([density[None], flow_vars], axis=0)
    from_next = passed_along(raw[:, :reach], AZ, -1)
    carried = carry(raw)
    ahead = carry(from_next[:, :MAXOFF])
    early = carry(lax.dynamic_slice_in_dim(raw, own_offset, cells - MAXOFF, 1))
    late = lax.dynamic_slice_in_dim(
        jnp.concatenate([carried[:, cells - MAXOFF :], ahead], axis=1), own_offset, MAXOFF, 1
    )
    early_sums = lax.psum(early, "blade")
    late_sums = ring_sum(late)
    sector_part = jnp.concatenate([early_sums, late_sums], axis=1)
    last = jnp.concatenate([early_sums[:, cells - MAXOFF - reach :], late_sums], axis=1)
    tail_sums = lax.dynamic_slice_in_dim(last, MAXOFF - own_offset, reach, 1)
    tail_means = tail_sums[1:4] / tail_sums[0:1]
    tail_fluctuation = velocity[:, cells - reach :] - tail_means
    fields = sector_part.shape[0]
    behind = passed_along(late_sums, AZ, 1)
    prev_fluctuation = passed_along(tail_fluctuation, AZ, 1)
    next_part = passed_along(early_sums[0:4, :reach], AZ, -1)
    own_sums = lax.dynamic_slice_in_dim(
        jnp.concatenate([behind, sector_part], axis=1), MAXOFF - own_offset, cells, 1
    )
    mean_fields = jnp.concatenate(
        [own_sums[0:1] / BLADES, own_sums[1:4] / own_sums[0:1], own_sums[4:5] / BLADES], axis=0
    )
    head_sums = lax.dynamic_slice_in_dim(
        jnp.concatenate([late_sums[0:4], next_part], axis=1),
        MAXOFF - next_offset,
        reach,
        1,
    )
    head_fluctuation = from_next[1:4] - head_sums[1:4] / head_sums[0:1]
    fluctuation = jnp.concatenate(
        [prev_fluctuation, velocity - mean_fields[1:4], head_fluctuation], axis=1
    )
    taps = smoothing_taps(smooth_width)
    rimmed = apply_taps(fluctuation, taps, cells + 2)
    smoothed = rimmed[:, 1 : cells + 1]
    rad_side = rad_rim(
        smoothed,
        jnp.concatenate([fluctuation[:, :, :1], fluctuation[:, :, -1:]], axis=2),
        taps,
        cells,
    )
    dtheta = 2.0 * math.pi / (cells * lax.axis_size(AZ))
    az_rate = (rimmed[:, 2:] - rimmed[:, :-2]) / (2.0 * dtheta)
    total_rad = rad_cells * lax.axis_size("rad")
    rows = lax.axis_index("rad") * rad_cells + jnp.arange(rad_cells)
    upper = jnp.where((rows == total_rad - 1)[:, None], smoothed, rad_side[:, :, 2:])
    lower = jnp.where((rows == 0)[:, None], smoothed, rad_side[:, :, :-2])
    span = jnp.where((rows == 0) | (rows == total_rad - 1), 1.0, 2.0).astype(jnp.float32)
    radial_rate = (upper - lower) / span[:, None]
    axial_rate = edge_rate(smoothed, 3)
    radius = (total_rad / 2 + rows.astype(jnp.float32) + 0.5)[:, None]
    q_field = swirl_measure(smoothed, az_rate, radial_rate, axial_rate, radius)
    return (mean_fields, q_field)


def solution(mesh):
    az, rad = mesh.devices.shape
    split = jax.sharding.Mesh(mesh.devices.reshape(BLADES, az // BLADES, rad), ("blade", "slab", "rad"))
    in_specs = (P(AZ, "rad", None), P(None, AZ, "rad", None), P(), P())
    out_specs = (P(None, AZ, "rad", None), P(AZ, "rad", None))
    return jax.shard_map(shards, mesh=split, in_specs=in_specs, out_specs=out_specs, check_vma=False)
```

```python
import math

import jax
import jax.numpy as jnp
from jax import lax
from jax.sharding import PartitionSpec as P

BLADES = 4
MAXOFF = 4
HW = 4
AZ = ("blade", "slab")


def passed_along(block, axis, distance):
    devices = range(lax.axis_size(axis))
    route = [((i - distance) % len(devices), i) for i in devices]
    return lax.ppermute(block, axis, route)


def extended(block, sides, width, periodic):
    for axis, dim in sides:
        count = lax.axis_size(axis)
        forward = [(i, i + 1) for i in range(count - 1)]
        if periodic:
            forward.append((count - 1, 0))
        backward = [(target, source) for source, target in forward]
        low = lax.ppermute(
            lax.slice_in_dim(block, block.shape[dim] - width, None, axis=dim), axis, forward
        )
        high = lax.ppermute(lax.slice_in_dim(block, 0, width, axis=dim), axis, backward)
        block = jnp.concatenate([low, block, high], axis=dim)
    return block


def ring_half(block, step):
    count = lax.axis_size("blade")
    place = lax.axis_index("blade")
    route = [(i, (i + step) % count) for i in range(count)]
    width = block.shape[1] // count
    doubled = jnp.concatenate([block, block], axis=1)

    def piece(index):
        return lax.dynamic_slice_in_dim(doubled, index * width, width, 1)

    total = piece(place % count)
    for turn in range(1, count):
        total = lax.ppermute(total, "blade", route) + piece((place - step * turn) % count)
    pieces = [total]
    for turn in range(1, count):
        pieces.append(lax.ppermute(pieces[-1], "blade", route))
    if step > 0:
        sequence, first = pieces[::-1], (place - 2) % count
    else:
        sequence, first = pieces, (place - 1) % count
    ordered = jnp.concatenate(sequence * 2, axis=1)
    return lax.dynamic_slice_in_dim(ordered, ((count - first) % count) * width, block.shape[1], 1)


def ring_sum(block):
    count = lax.axis_size("blade")
    half = block.shape[1] // 2
    parts = []
    for step, part in ((1, block[:, :half]), (-1, block[:, half:])):
        shape = part.shape
        if shape[1] % count:
            part = part.reshape(shape[0], shape[1] * 2, shape[2] // 2, shape[3])
        parts.append(ring_half(part, step).reshape(shape))
    return jnp.concatenate(parts, axis=1)


def rad_rim(block, edges, taps, cells):
    count = lax.axis_size("rad")
    forward = [(i, i + 1) for i in range(count - 1)]
    backward = [(target, source) for source, target in forward]
    edge_rows = apply_taps(edges, taps, cells + 2)[:, 1 : cells + 1]
    low = lax.ppermute(edge_rows[:, :, 1], "rad", forward)
    high = lax.ppermute(edge_rows[:, :, 0], "rad", backward)
    return jnp.concatenate([low[:, :, None], block, high[:, :, None]], axis=2)


def smoothing_taps(smooth_width):
    spread = jnp.arange(-HW, HW + 1)
    width = smooth_width.astype(jnp.float32)
    square = (spread.astype(jnp.float32) ** 2)[:, None]
    weights = jnp.where(
        jnp.abs(spread)[:, None] <= smooth_width[None, :],
        jnp.exp(-0.5 * square / (width * width)[None, :]),
        0.0,
    )
    return weights / jnp.sum(weights, axis=0, keepdims=True)


def apply_taps(source, taps, length):
    total = jnp.zeros(source.shape[:1] + (length,) + source.shape[2:], jnp.float32)
    for turn in range(2 * HW + 1):
        total = total + taps[turn] * source[:, turn : turn + length]
    return total


def edge_rate(field, axis):
    count = field.shape[axis]
    upper = jnp.concatenate(
        [
            lax.slice_in_dim(field, 1, count, axis=axis),
            lax.slice_in_dim(field, count - 1, count, axis=axis),
        ],
        axis=axis,
    )
    lower = jnp.concatenate(
        [
            lax.slice_in_dim(field, 0, 1, axis=axis),
            lax.slice_in_dim(field, 0, count - 1, axis=axis),
        ],
        axis=axis,
    )
    places = jnp.arange(count)
    span = jnp.where((places == 0) | (places == count - 1), 1.0, 2.0).astype(field.dtype)
    layout = [1] * field.ndim
    layout[axis] = count
    return (upper - lower) / span.reshape(layout)


def swirl_measure(smoothed, az_rate, radial_rate, axial_rate, radius):
    tensor_aa = radial_rate[0]
    tensor_ab = (az_rate[0] - smoothed[1]) / radius
    tensor_ac = axial_rate[0]
    tensor_ba = radial_rate[1]
    tensor_bb = (az_rate[1] + smoothed[0]) / radius
    tensor_bc = axial_rate[1]
    tensor_ca = radial_rate[2]
    tensor_cb = az_rate[2] / radius
    tensor_cc = axial_rate[2]
    diagonal_part = tensor_aa * tensor_aa + tensor_bb * tensor_bb + tensor_cc * tensor_cc
    cross_part = tensor_ab * tensor_ba + tensor_ac * tensor_ca + tensor_bc * tensor_cb
    return -0.5 * (diagonal_part + 2.0 * cross_part)


def carry(raw):
    return jnp.concatenate([raw[0:1], raw[0:1] * raw[1:4], raw[4:5]], axis=0)


def shards(density, flow_vars, blade_offset, smooth_width):
    cells = density.shape[0]
    rad_cells = density.shape[1]
    group = lax.axis_size("slab")
    blade = lax.axis_index("blade")
    slab = lax.axis_index("slab")

    def offset_of(which):
        return jnp.sum(jnp.where(jnp.arange(BLADES) == which, blade_offset, 0))

    own_offset = offset_of(blade)
    next_offset = offset_of(jnp.where(slab == group - 1, (blade + 1) % BLADES, blade))
    reach = HW + 1
    velocity = flow_vars[0:3]
    raw = jnp.concatenate([density[None], flow_vars], axis=0)
    ahead_raw = passed_along(raw[:, :MAXOFF], AZ, -1)
    extra = passed_along(velocity[:, MAXOFF:reach], AZ, -1)
    next_velocity = jnp.concatenate([ahead_raw[1:4], extra], axis=1)
    carried = carry(raw)
    ahead = carry(ahead_raw)
    early = carry(lax.dynamic_slice_in_dim(raw, own_offset, cells - MAXOFF, 1))
    late = lax.dynamic_slice_in_dim(
        jnp.concatenate([carried[:, cells - MAXOFF :], ahead], axis=1), own_offset, MAXOFF, 1
    )
    early_sums = lax.psum(early, "blade")
    late_sums = ring_sum(late)
    sector_part = jnp.concatenate([early_sums, late_sums], axis=1)
    last = jnp.concatenate([early_sums[:, cells - MAXOFF - reach :], late_sums], axis=1)
    tail_sums = lax.dynamic_slice_in_dim(last, MAXOFF - own_offset, reach, 1)
    tail_means = tail_sums[1:4] / tail_sums[0:1]
    tail_fluctuation = velocity[:, cells - reach :] - tail_means
    fields = sector_part.shape[0]
    behind = passed_along(late_sums, AZ, 1)
    prev_fluctuation = passed_along(tail_fluctuation, AZ, 1)
    next_part = passed_along(early_sums[0:4, :reach], AZ, -1)
    own_sums = lax.dynamic_slice_in_dim(
        jnp.concatenate([behind, sector_part], axis=1), MAXOFF - own_offset, cells, 1
    )
    mean_fields = jnp.concatenate(
        [own_sums[0:1] / BLADES, own_sums[1:4] / own_sums[0:1], own_sums[4:5] / BLADES], axis=0
    )
    head_sums = lax.dynamic_slice_in_dim(
        jnp.concatenate([late_sums[0:4], next_part], axis=1),
        MAXOFF - next_offset,
        reach,
        1,
    )
    head_fluctuation = next_velocity - head_sums[1:4] / head_sums[0:1]
    fluctuation = jnp.concatenate(
        [prev_fluctuation, velocity - mean_fields[1:4], head_fluctuation], axis=1
    )
    taps = smoothing_taps(smooth_width)
    rimmed = apply_taps(fluctuation, taps, cells + 2)
    smoothed = rimmed[:, 1 : cells + 1]
    rad_side = rad_rim(
        smoothed,
        jnp.concatenate([fluctuation[:, :, :1], fluctuation[:, :, -1:]], axis=2),
        taps,
        cells,
    )
    dtheta = 2.0 * math.pi / (cells * lax.axis_size(AZ))
    az_rate = (rimmed[:, 2:] - rimmed[:, :-2]) / (2.0 * dtheta)
    total_rad = rad_cells * lax.axis_size("rad")
    rows = lax.axis_index("rad") * rad_cells + jnp.arange(rad_cells)
    upper = jnp.where((rows == total_rad - 1)[:, None], smoothed, rad_side[:, :, 2:])
    lower = jnp.where((rows == 0)[:, None], smoothed, rad_side[:, :, :-2])
    span = jnp.where((rows == 0) | (rows == total_rad - 1), 1.0, 2.0).astype(jnp.float32)
    radial_rate = (upper - lower) / span[:, None]
    axial_rate = edge_rate(smoothed, 3)
    radius = (total_rad / 2 + rows.astype(jnp.float32) + 0.5)[:, None]
    q_field = swirl_measure(smoothed, az_rate, radial_rate, axial_rate, radius)
    return (mean_fields, q_field)


def solution(mesh):
    az, rad = mesh.devices.shape
    split = jax.sharding.Mesh(mesh.devices.reshape(BLADES, az // BLADES, rad), ("blade", "slab", "rad"))
    in_specs = (P(AZ, "rad", None), P(None, AZ, "rad", None), P(), P())
    out_specs = (P(None, AZ, "rad", None), P(AZ, "rad", None))
    return jax.shard_map(shards, mesh=split, in_specs=in_specs, out_specs=out_specs, check_vma=False)
```

```python
import math

import jax
import jax.numpy as jnp
from jax import lax
from jax.sharding import PartitionSpec as P

BLADES = 4
MAXOFF = 4
HW = 4
AZ = ("blade", "slab")


def passed_along(block, axis, distance):
    devices = range(lax.axis_size(axis))
    route = [((i - distance) % len(devices), i) for i in devices]
    return lax.ppermute(block, axis, route)


def extended(block, sides, width, periodic):
    for axis, dim in sides:
        count = lax.axis_size(axis)
        forward = [(i, i + 1) for i in range(count - 1)]
        if periodic:
            forward.append((count - 1, 0))
        backward = [(target, source) for source, target in forward]
        low = lax.ppermute(
            lax.slice_in_dim(block, block.shape[dim] - width, None, axis=dim), axis, forward
        )
        high = lax.ppermute(lax.slice_in_dim(block, 0, width, axis=dim), axis, backward)
        block = jnp.concatenate([low, block, high], axis=dim)
    return block


def ring_half(block, step):
    count = lax.axis_size("blade")
    place = lax.axis_index("blade")
    route = [(i, (i + step) % count) for i in range(count)]
    width = block.shape[1] // count
    doubled = jnp.concatenate([block, block], axis=1)

    def piece(index):
        return lax.dynamic_slice_in_dim(doubled, index * width, width, 1)

    total = piece(place % count)
    for turn in range(1, count):
        total = lax.ppermute(total, "blade", route) + piece((place - step * turn) % count)
    pieces = [total]
    for turn in range(1, count):
        pieces.append(lax.ppermute(pieces[-1], "blade", route))
    if step > 0:
        sequence, first = pieces[::-1], (place - 2) % count
    else:
        sequence, first = pieces, (place - 1) % count
    ordered = jnp.concatenate(sequence * 2, axis=1)
    return lax.dynamic_slice_in_dim(ordered, ((count - first) % count) * width, block.shape[1], 1)


def ring_sum(block):
    count = lax.axis_size("blade")
    half = block.shape[1] // 2
    parts = []
    for step, part in ((1, block[:, :half]), (-1, block[:, half:])):
        shape = part.shape
        if shape[1] % count:
            part = part.reshape(shape[0], shape[1] * 2, shape[2] // 2, shape[3])
        parts.append(ring_half(part, step).reshape(shape))
    return jnp.concatenate(parts, axis=1)


def rad_rim(block, edges, taps, cells):
    count = lax.axis_size("rad")
    forward = [(i, i + 1) for i in range(count - 1)]
    backward = [(target, source) for source, target in forward]
    edge_rows = apply_taps(edges, taps, cells + 2)[:, 1 : cells + 1]
    low = lax.ppermute(edge_rows[:, :, 1], "rad", forward)
    high = lax.ppermute(edge_rows[:, :, 0], "rad", backward)
    return jnp.concatenate([low[:, :, None], block, high[:, :, None]], axis=2)


def smoothing_taps(smooth_width):
    spread = jnp.arange(-HW, HW + 1)
    width = smooth_width.astype(jnp.float32)
    square = (spread.astype(jnp.float32) ** 2)[:, None]
    weights = jnp.where(
        jnp.abs(spread)[:, None] <= smooth_width[None, :],
        jnp.exp(-0.5 * square / (width * width)[None, :]),
        0.0,
    )
    return weights / jnp.sum(weights, axis=0, keepdims=True)


def apply_taps(source, taps, length):
    total = jnp.zeros(source.shape[:1] + (length,) + source.shape[2:], jnp.float32)
    for turn in range(2 * HW + 1):
        total = total + taps[turn] * source[:, turn : turn + length]
    return total


def edge_rate(field, axis):
    count = field.shape[axis]
    upper = jnp.concatenate(
        [
            lax.slice_in_dim(field, 1, count, axis=axis),
            lax.slice_in_dim(field, count - 1, count, axis=axis),
        ],
        axis=axis,
    )
    lower = jnp.concatenate(
        [
            lax.slice_in_dim(field, 0, 1, axis=axis),
            lax.slice_in_dim(field, 0, count - 1, axis=axis),
        ],
        axis=axis,
    )
    places = jnp.arange(count)
    span = jnp.where((places == 0) | (places == count - 1), 1.0, 2.0).astype(field.dtype)
    layout = [1] * field.ndim
    layout[axis] = count
    return (upper - lower) / span.reshape(layout)


def swirl_measure(smoothed, az_rate, radial_rate, axial_rate, radius):
    tensor_aa = radial_rate[0]
    tensor_ab = (az_rate[0] - smoothed[1]) / radius
    tensor_ac = axial_rate[0]
    tensor_ba = radial_rate[1]
    tensor_bb = (az_rate[1] + smoothed[0]) / radius
    tensor_bc = axial_rate[1]
    tensor_ca = radial_rate[2]
    tensor_cb = az_rate[2] / radius
    tensor_cc = axial_rate[2]
    diagonal_part = tensor_aa * tensor_aa + tensor_bb * tensor_bb + tensor_cc * tensor_cc
    cross_part = tensor_ab * tensor_ba + tensor_ac * tensor_ca + tensor_bc * tensor_cb
    return -0.5 * (diagonal_part + 2.0 * cross_part)


def carry(raw):
    return jnp.concatenate([raw[0:1], raw[0:1] * raw[1:4], raw[4:5]], axis=0)


def shards(density, flow_vars, blade_offset, smooth_width):
    cells = density.shape[0]
    rad_cells = density.shape[1]
    group = lax.axis_size("slab")
    blade = lax.axis_index("blade")
    slab = lax.axis_index("slab")

    def offset_of(which):
        return jnp.sum(jnp.where(jnp.arange(BLADES) == which, blade_offset, 0))

    own_offset = offset_of(blade)
    next_offset = offset_of(jnp.where(slab == group - 1, (blade + 1) % BLADES, blade))
    reach = HW + 1
    velocity = flow_vars[0:3]
    raw = jnp.concatenate([density[None], flow_vars], axis=0)
    from_next = passed_along(raw[:, :reach], AZ, -1)
    carried = carry(raw)
    ahead = carry(from_next[:, :MAXOFF])
    early = carry(lax.dynamic_slice_in_dim(raw, own_offset, cells - MAXOFF, 1))
    late = lax.dynamic_slice_in_dim(
        jnp.concatenate([carried[:, cells - MAXOFF :], ahead], axis=1), own_offset, MAXOFF, 1
    )
    early_sums = lax.psum(early, "blade")
    late_sums = ring_half(late, 1)
    sector_part = jnp.concatenate([early_sums, late_sums], axis=1)
    last = jnp.concatenate([early_sums[:, cells - MAXOFF - reach :], late_sums], axis=1)
    tail_sums = lax.dynamic_slice_in_dim(last, MAXOFF - own_offset, reach, 1)
    tail_means = tail_sums[1:4] / tail_sums[0:1]
    tail_fluctuation = velocity[:, cells - reach :] - tail_means
    fields = sector_part.shape[0]
    behind = passed_along(late_sums, AZ, 1)
    prev_fluctuation = passed_along(tail_fluctuation, AZ, 1)
    next_part = passed_along(early_sums[0:4, :reach], AZ, -1)
    own_sums = lax.dynamic_slice_in_dim(
        jnp.concatenate([behind, sector_part], axis=1), MAXOFF - own_offset, cells, 1
    )
    mean_fields = jnp.concatenate(
        [own_sums[0:1] / BLADES, own_sums[1:4] / own_sums[0:1], own_sums[4:5] / BLADES], axis=0
    )
    head_sums = lax.dynamic_slice_in_dim(
        jnp.concatenate([late_sums[0:4], next_part], axis=1),
        MAXOFF - next_offset,
        reach,
        1,
    )
    head_fluctuation = from_next[1:4] - head_sums[1:4] / head_sums[0:1]
    fluctuation = jnp.concatenate(
        [prev_fluctuation, velocity - mean_fields[1:4], head_fluctuation], axis=1
    )
    taps = smoothing_taps(smooth_width)
    rimmed = apply_taps(fluctuation, taps, cells + 2)
    smoothed = rimmed[:, 1 : cells + 1]
    rad_side = rad_rim(
        smoothed,
        jnp.concatenate([fluctuation[:, :, :1], fluctuation[:, :, -1:]], axis=2),
        taps,
        cells,
    )
    dtheta = 2.0 * math.pi / (cells * lax.axis_size(AZ))
    az_rate = (rimmed[:, 2:] - rimmed[:, :-2]) / (2.0 * dtheta)
    total_rad = rad_cells * lax.axis_size("rad")
    rows = lax.axis_index("rad") * rad_cells + jnp.arange(rad_cells)
    upper = jnp.where((rows == total_rad - 1)[:, None], smoothed, rad_side[:, :, 2:])
    lower = jnp.where((rows == 0)[:, None], smoothed, rad_side[:, :, :-2])
    span = jnp.where((rows == 0) | (rows == total_rad - 1), 1.0, 2.0).astype(jnp.float32)
    radial_rate = (upper - lower) / span[:, None]
    axial_rate = edge_rate(smoothed, 3)
    radius = (total_rad / 2 + rows.astype(jnp.float32) + 0.5)[:, None]
    q_field = swirl_measure(smoothed, az_rate, radial_rate, axial_rate, radius)
    return (mean_fields, q_field)


def solution(mesh):
    az, rad = mesh.devices.shape
    split = jax.sharding.Mesh(mesh.devices.reshape(BLADES, az // BLADES, rad), ("blade", "slab", "rad"))
    in_specs = (P(AZ, "rad", None), P(None, AZ, "rad", None), P(), P())
    out_specs = (P(None, AZ, "rad", None), P(AZ, "rad", None))
    return jax.shard_map(shards, mesh=split, in_specs=in_specs, out_specs=out_specs, check_vma=False)
```

```python
import math

import jax
import jax.numpy as jnp
from jax import lax
from jax.sharding import PartitionSpec as P

BLADES = 4
MAXOFF = 4
HW = 4
AZ = ("blade", "slab")


def passed_along(block, axis, distance):
    devices = range(lax.axis_size(axis))
    route = [((i - distance) % len(devices), i) for i in devices]
    return lax.ppermute(block, axis, route)


def extended(block, sides, width, periodic):
    for axis, dim in sides:
        count = lax.axis_size(axis)
        forward = [(i, i + 1) for i in range(count - 1)]
        if periodic:
            forward.append((count - 1, 0))
        backward = [(target, source) for source, target in forward]
        low = lax.ppermute(
            lax.slice_in_dim(block, block.shape[dim] - width, None, axis=dim), axis, forward
        )
        high = lax.ppermute(lax.slice_in_dim(block, 0, width, axis=dim), axis, backward)
        block = jnp.concatenate([low, block, high], axis=dim)
    return block


def ring_half(block, step):
    count = lax.axis_size("blade")
    place = lax.axis_index("blade")
    route = [(i, (i + step) % count) for i in range(count)]
    width = block.shape[1] // count
    doubled = jnp.concatenate([block, block], axis=1)

    def piece(index):
        return lax.dynamic_slice_in_dim(doubled, index * width, width, 1)

    total = piece(place % count)
    for turn in range(1, count):
        total = lax.ppermute(total, "blade", route) + piece((place - step * turn) % count)
    pieces = [total]
    for turn in range(1, count):
        pieces.append(lax.ppermute(pieces[-1], "blade", route))
    if step > 0:
        sequence, first = pieces[::-1], (place - 2) % count
    else:
        sequence, first = pieces, (place - 1) % count
    ordered = jnp.concatenate(sequence * 2, axis=1)
    return lax.dynamic_slice_in_dim(ordered, ((count - first) % count) * width, block.shape[1], 1)


def ring_sum(block):
    count = lax.axis_size("blade")
    half = block.shape[1] // 2
    parts = []
    for step, part in ((1, block[:, :half]), (-1, block[:, half:])):
        shape = part.shape
        if shape[1] % count:
            part = part.reshape(shape[0], shape[1] * 2, shape[2] // 2, shape[3])
        parts.append(ring_half(part, step).reshape(shape))
    return jnp.concatenate(parts, axis=1)


def rad_rim(block, edges, taps, cells):
    count = lax.axis_size("rad")
    forward = [(i, i + 1) for i in range(count - 1)]
    backward = [(target, source) for source, target in forward]
    edge_rows = apply_taps(edges, taps, cells + 2)[:, 1 : cells + 1]
    low = lax.ppermute(edge_rows[:, :, 1], "rad", forward)
    high = lax.ppermute(edge_rows[:, :, 0], "rad", backward)
    return jnp.concatenate([low[:, :, None], block, high[:, :, None]], axis=2)


def smoothing_taps(smooth_width):
    spread = jnp.arange(-HW, HW + 1)
    width = smooth_width.astype(jnp.float32)
    square = (spread.astype(jnp.float32) ** 2)[:, None]
    weights = jnp.where(
        jnp.abs(spread)[:, None] <= smooth_width[None, :],
        jnp.exp(-0.5 * square / (width * width)[None, :]),
        0.0,
    )
    return weights / jnp.sum(weights, axis=0, keepdims=True)


def apply_taps(source, taps, length):
    total = jnp.zeros(source.shape[:1] + (length,) + source.shape[2:], jnp.float32)
    for turn in range(2 * HW + 1):
        total = total + taps[turn] * source[:, turn : turn + length]
    return total


def edge_rate(field, axis):
    count = field.shape[axis]
    upper = jnp.concatenate(
        [
            lax.slice_in_dim(field, 1, count, axis=axis),
            lax.slice_in_dim(field, count - 1, count, axis=axis),
        ],
        axis=axis,
    )
    lower = jnp.concatenate(
        [
            lax.slice_in_dim(field, 0, 1, axis=axis),
            lax.slice_in_dim(field, 0, count - 1, axis=axis),
        ],
        axis=axis,
    )
    places = jnp.arange(count)
    span = jnp.where((places == 0) | (places == count - 1), 1.0, 2.0).astype(field.dtype)
    layout = [1] * field.ndim
    layout[axis] = count
    return (upper - lower) / span.reshape(layout)


def swirl_measure(smoothed, az_rate, radial_rate, axial_rate, radius):
    tensor_aa = radial_rate[0]
    tensor_ab = (az_rate[0] - smoothed[1]) / radius
    tensor_ac = axial_rate[0]
    tensor_ba = radial_rate[1]
    tensor_bb = (az_rate[1] + smoothed[0]) / radius
    tensor_bc = axial_rate[1]
    tensor_ca = radial_rate[2]
    tensor_cb = az_rate[2] / radius
    tensor_cc = axial_rate[2]
    diagonal_part = tensor_aa * tensor_aa + tensor_bb * tensor_bb + tensor_cc * tensor_cc
    cross_part = tensor_ab * tensor_ba + tensor_ac * tensor_ca + tensor_bc * tensor_cb
    return -0.5 * (diagonal_part + 2.0 * cross_part)


def carry(raw):
    return jnp.concatenate([raw[0:1], raw[0:1] * raw[1:4], raw[4:5]], axis=0)


def shards(density, flow_vars, blade_offset, smooth_width):
    cells = density.shape[0]
    rad_cells = density.shape[1]
    group = lax.axis_size("slab")
    blade = lax.axis_index("blade")
    slab = lax.axis_index("slab")

    def offset_of(which):
        return jnp.sum(jnp.where(jnp.arange(BLADES) == which, blade_offset, 0))

    own_offset = offset_of(blade)
    next_offset = offset_of(jnp.where(slab == group - 1, (blade + 1) % BLADES, blade))
    reach = HW + 1
    velocity = flow_vars[0:3]
    raw = jnp.concatenate([density[None], flow_vars], axis=0)
    from_next = passed_along(raw[:, :MAXOFF], AZ, -1)
    carried = carry(raw)
    ahead = carry(from_next)
    early = carry(lax.dynamic_slice_in_dim(raw, own_offset, cells - MAXOFF, 1))
    late = lax.dynamic_slice_in_dim(
        jnp.concatenate([carried[:, cells - MAXOFF :], ahead], axis=1), own_offset, MAXOFF, 1
    )
    early_sums = lax.psum(early, "blade")
    late_sums = ring_sum(late)
    sector_part = jnp.concatenate([early_sums, late_sums], axis=1)
    last = jnp.concatenate([early_sums[:, cells - MAXOFF - reach :], late_sums], axis=1)
    tail_sums = lax.dynamic_slice_in_dim(last, MAXOFF - own_offset, reach, 1)
    tail_means = tail_sums[1:4] / tail_sums[0:1]
    tail_fluctuation = velocity[:, cells - reach :] - tail_means
    fields = sector_part.shape[0]
    behind = passed_along(late_sums, AZ, 1)
    prev_fluctuation = passed_along(tail_fluctuation, AZ, 1)
    own_sums = lax.dynamic_slice_in_dim(
        jnp.concatenate([behind, sector_part], axis=1), MAXOFF - own_offset, cells, 1
    )
    mean_fields = jnp.concatenate(
        [own_sums[0:1] / BLADES, own_sums[1:4] / own_sums[0:1], own_sums[4:5] / BLADES], axis=0
    )
    own_fluctuation = velocity - mean_fields[1:4]
    head_fluctuation = passed_along(own_fluctuation[:, :reach], AZ, -1)
    fluctuation = jnp.concatenate([prev_fluctuation, own_fluctuation, head_fluctuation], axis=1)
    taps = smoothing_taps(smooth_width)
    rimmed = apply_taps(fluctuation, taps, cells + 2)
    smoothed = rimmed[:, 1 : cells + 1]
    rad_side = rad_rim(
        smoothed,
        jnp.concatenate([fluctuation[:, :, :1], fluctuation[:, :, -1:]], axis=2),
        taps,
        cells,
    )
    dtheta = 2.0 * math.pi / (cells * lax.axis_size(AZ))
    az_rate = (rimmed[:, 2:] - rimmed[:, :-2]) / (2.0 * dtheta)
    total_rad = rad_cells * lax.axis_size("rad")
    rows = lax.axis_index("rad") * rad_cells + jnp.arange(rad_cells)
    upper = jnp.where((rows == total_rad - 1)[:, None], smoothed, rad_side[:, :, 2:])
    lower = jnp.where((rows == 0)[:, None], smoothed, rad_side[:, :, :-2])
    span = jnp.where((rows == 0) | (rows == total_rad - 1), 1.0, 2.0).astype(jnp.float32)
    radial_rate = (upper - lower) / span[:, None]
    axial_rate = edge_rate(smoothed, 3)
    radius = (total_rad / 2 + rows.astype(jnp.float32) + 0.5)[:, None]
    q_field = swirl_measure(smoothed, az_rate, radial_rate, axial_rate, radius)
    return (mean_fields, q_field)


def solution(mesh):
    az, rad = mesh.devices.shape
    split = jax.sharding.Mesh(mesh.devices.reshape(BLADES, az // BLADES, rad), ("blade", "slab", "rad"))
    in_specs = (P(AZ, "rad", None), P(None, AZ, "rad", None), P(), P())
    out_specs = (P(None, AZ, "rad", None), P(AZ, "rad", None))
    return jax.shard_map(shards, mesh=split, in_specs=in_specs, out_specs=out_specs, check_vma=False)
```
